32 devices in a mesh: groups: 2 (over y), tm: 4 (over x, core), width: 4 (over z).
Axes of the slice: x: 2, y: 2, z: 4, core: 2. Of those that a mesh axis runs over, the one named last changes fastest.
Arguments:
- video: bfloat16 [32, 12, 48, 256], P(('groups', 'tm'), None, 'width'), parts along dimension 0, may hold values from -6 to 6
- conv_w: bfloat16 [2, 3, 3, 256, 256], replicated, may hold values from -0.125 to 0.125
- depth_k: float32 [2, 16, 256], replicated, may hold values from -1.5 to 1.5
- proj_w: bfloat16 [2, 256, 256], replicated, may hold values from -0.375 to 0.375
Outputs:
- result: bfloat16 [32, 12, 48, 256], P(('groups', 'tm'), None, 'width'), parts along dimension 0
The draws below stay inside these ranges and needn't reach their ends.
There are 2 independent parts, one for each index of `groups`. The reference program is written for one: setup_inputs(seed, part) draws one part's arguments, and reference() takes and returns one part's arrays. A program takes and returns all parts, laid end to end along the dimension named above; an argument that names none is the same for every part. Nothing has to cross between parts.
All inputs are finite; a program needn't handle non-finite values.
Results may differ from the reference program's by a relative error of at most 0.0058.
Values may be sent and summed in bfloat16 or wider, within the bound.
No kernel may reach another device: no remote copies, remote signals or barrier semaphores. Data moves between devices by JAX's collectives and lax.ppermute only.
A program may use at most 64 MiB of HBM per device.

```python
import jax
import jax.numpy as jnp
from jax import lax

C = 256
F = 16
BLOCKS = 2
H = 12
W = 48


def level_of(stream_key, extent, shards, least, high):
    def one(position, blocks):
        draws = jax.random.uniform(jax.random.fold_in(jax.random.fold_in(stream_key, 6), position), (blocks,), jnp.float32, least / len(shards), high / len(shards))
        return jnp.repeat(jnp.exp(draws), extent[position] // blocks).reshape((-1,) + (1,) * (len(extent) - position - 1))

    factor_of = one(*shards[0])
    for cut in shards[1:]:
        factor_of = factor_of * one(*cut)
    return factor_of


def scatter_about(stream_key, extent, deviation, bound, split=(), held_as=jnp.bfloat16):
    entries = jax.random.normal(stream_key, extent, jnp.float32) * deviation
    if len(split) > 0:
        entries = level_of(stream_key, extent, split, -0.22, 0.18) * entries
    return jnp.clip(entries, min=-bound, max=bound).astype(held_as)


def setup_inputs(seed: int = 0, part: int = 0) -> dict:
    key_of = jax.random.split(jax.random.key(seed), 5)
    own_keys = jax.random.split(jax.random.fold_in(key_of[4], part), 5)
    video = scatter_about(own_keys[0], (F, H, W, C), 1.0, 6.0, ((0, 4), (2, 4)))
    conv_w = scatter_about(key_of[1], (BLOCKS, 3, 3, C, C), (9 * C) ** -0.5, 0.125)
    depth_k = scatter_about(key_of[2], (BLOCKS, F, C), F ** -0.5, 1.5, (), jnp.float32)
    proj_w = scatter_about(key_of[3], (BLOCKS, C, C), C ** -0.5, 0.375)
    return dict(video=video, conv_w=conv_w, depth_k=depth_k, proj_w=proj_w)


def spatial(state, weight):
    frames, rows, cols, chans = state.shape
    padded = jnp.pad(state, ((0, 0), (1, 1), (1, 1), (0, 0)))
    total = jnp.zeros((frames * rows * cols, chans), jnp.float32)
    for dy in range(3):
        for dx in range(3):
            piece = padded[:, dy:dy + rows, dx:dx + cols, :].reshape(-1, chans)
            total = total + jnp.dot(piece, weight[dy, dx], preferred_element_type=jnp.float32)
    return total.reshape(frames, rows, cols, chans)


def temporal(hidden, kernel, proj):
    frames = hidden.shape[0]
    chans = hidden.shape[-1]
    later = jnp.arange(frames, dtype=jnp.int32)[:, None]
    earlier = jnp.arange(frames, dtype=jnp.int32)[None, :]
    offset = (later - earlier) % frames
    toeplitz = jnp.where((later >= earlier)[:, :, None], kernel[offset], jnp.zeros((), jnp.float32))
    values = hidden.astype(jnp.float32)
    total = jnp.einsum("tsc,sijc->tijc", toeplitz, values, precision=lax.Precision.HIGHEST)
    depth = total.astype(jnp.bfloat16)
    mixed = jnp.dot(depth.reshape(-1, chans), proj, preferred_element_type=jnp.float32)
    return mixed.reshape(hidden.shape).astype(jnp.bfloat16)


def reference(video, conv_w, depth_k, proj_w):
    state = video
    for block in range(BLOCKS):
        hidden = jax.nn.silu(spatial(state, conv_w[block])).astype(jnp.bfloat16)
        mixed = temporal(hidden, depth_k[block], proj_w[block])
        state = (state.astype(jnp.float32) + mixed.astype(jnp.float32)).astype(jnp.bfloat16)
    return state
```

```python
import jax
import jax.numpy as jnp
from jax import lax
from jax.sharding import PartitionSpec as P

BLOCKS = 2


def conv3x3(x, weight):
    return lax.conv_general_dilated(
        x,
        weight,
        window_strides=(1, 1),
        padding="VALID",
        dimension_numbers=("NHWC", "HWIO", "NHWC"),
        preferred_element_type=jnp.float32,
    )


def block(x, weight, kernel, proj):
    chans = x.shape[-1]
    hidden = jax.nn.silu(conv3x3(x, weight)).astype(jnp.bfloat16)
    frames = hidden.shape[0]
    values = hidden.astype(jnp.float32)
    depth = values * kernel[0]
    for lag in range(1, frames):
        shifted = jnp.pad(values[: frames - lag], ((lag, 0), (0, 0), (0, 0), (0, 0)))
        depth = depth + shifted * kernel[lag]
    depth = depth.astype(jnp.bfloat16)
    mixed = jnp.dot(depth.reshape(-1, chans), proj, preferred_element_type=jnp.float32)
    mixed = mixed.reshape(hidden.shape).astype(jnp.bfloat16)
    inner = x[:, 1:-1, 1:-1, :]
    return (inner.astype(jnp.float32) + mixed.astype(jnp.float32)).astype(jnp.bfloat16)


def shards(video, conv_w, depth_k, proj_w):
    bands = lax.axis_size("tm")
    sides = lax.axis_size("width")
    band = lax.axis_index("tm")
    side = lax.axis_index("width")
    frames, height, cols, chans = video.shape
    rows = height // bands
    halo = BLOCKS

    padded = jnp.pad(video, ((0, 0), (halo, halo), (0, 0), (0, 0)))
    pieces = jnp.stack([padded[:, r * rows : r * rows + rows + 2 * halo] for r in range(bands)])
    gathered = lax.all_to_all(pieces, "tm", 0, 0, tiled=False)
    gathered = gathered.reshape(bands * frames, rows + 2 * halo, cols, chans)

    up = [(i, i + 1) for i in range(sides - 1)]
    down = [(i + 1, i) for i in range(sides - 1)]
    before = lax.ppermute(gathered[:, :, cols - halo :], "width", up)
    after = lax.ppermute(gathered[:, :, :halo], "width", down)
    state = jnp.concatenate([before, gathered, after], axis=2)

    for b in range(BLOCKS):
        state = block(state, conv_w[b], depth_k[b], proj_w[b])
        left = halo - 1 - b
        if left > 0:
            n_rows, n_cols = state.shape[1], state.shape[2]
            row = band * rows - left + lax.broadcasted_iota(jnp.int32, (n_rows, n_cols), 0)
            col = side * cols - left + lax.broadcasted_iota(jnp.int32, (n_rows, n_cols), 1)
            inside = (row >= 0) & (row < height) & (col >= 0) & (col < sides * cols)
            state = jnp.where(inside[None, :, :, None], state, jnp.zeros((), state.dtype))

    return lax.all_to_all(state, "tm", 0, 1, tiled=True)


def solution(mesh):
    return jax.shard_map(
        shards,
        mesh=mesh,
        in_specs=(P(("groups", "tm"), None, "width", None), P(), P(), P()),
        out_specs=P(("groups", "tm"), None, "width", None),
        check_vma=False,
    )
```

```python
import jax
import jax.numpy as jnp
from jax import lax
from jax.sharding import PartitionSpec as P

BLOCKS = 2


def conv3x3(x, weight):
    return lax.conv_general_dilated(
        x,
        weight,
        window_strides=(1, 1),
        padding="VALID",
        dimension_numbers=("NHWC", "HWIO", "NHWC"),
        preferred_element_type=jnp.float32,
    )


def block(x, weight, kernel, proj):
    chans = x.shape[-1]
    hidden = jax.nn.silu(conv3x3(x, weight)).astype(jnp.bfloat16)
    frames = hidden.shape[0]
    values = hidden.astype(jnp.float32)
    depth = values * kernel[0]
    for lag in range(1, frames):
        shifted = jnp.pad(values[: frames - lag], ((lag, 0), (0, 0), (0, 0), (0, 0)))
        depth = depth + shifted * kernel[lag]
    depth = depth.astype(jnp.bfloat16)
    mixed = jnp.dot(depth.reshape(-1, chans), proj, preferred_element_type=jnp.float32)
    mixed = mixed.reshape(hidden.shape).astype(jnp.bfloat16)
    inner = x[:, 1:-1, 1:-1, :]
    return (inner.astype(jnp.float32) + mixed.astype(jnp.float32)).astype(jnp.bfloat16)


def shards(video, conv_w, depth_k, proj_w):
    bands = lax.axis_size("tm")
    sides = lax.axis_size("width")
    band = lax.axis_index("tm")
    side = lax.axis_index("width")
    frames, height, cols, chans = video.shape
    rows = height // bands
    halo = BLOCKS

    padded = jnp.pad(video, ((0, 0), (halo, halo), (0, 0), (0, 0)))
    starts = [r * rows for r in range(bands)]
    pieces = jnp.stack([padded[:, s : s + rows + 2 * halo] for s in starts])
    gathered = lax.all_to_all(pieces, "tm", 0, 0, tiled=False)
    gathered = gathered.reshape(bands * frames, rows + 2 * halo, cols, chans)

    target = lax.broadcasted_iota(jnp.int32, (1, sides, 1, 1, 1, 1), 1)
    lead = pieces[:, :, :, :halo]
    tail = pieces[:, :, :, cols - halo :]
    zero = jnp.zeros((), pieces.dtype)
    edges = jnp.where(target == side + 1, tail[:, None], jnp.where(target == side - 1, lead[:, None], zero))
    edges = edges.reshape((bands * sides,) + edges.shape[2:])
    edges = lax.all_to_all(edges, ("tm", "width"), 0, 0, tiled=False)
    edges = edges.reshape((bands, sides) + edges.shape[1:])
    before = lax.dynamic_index_in_dim(edges, jnp.maximum(side - 1, 0), axis=1, keepdims=False)
    after = lax.dynamic_index_in_dim(edges, jnp.minimum(side + 1, sides - 1), axis=1, keepdims=False)
    before = jnp.where(side > 0, before, zero).reshape(bands * frames, rows + 2 * halo, halo, chans)
    after = jnp.where(side < sides - 1, after, zero).reshape(bands * frames, rows + 2 * halo, halo, chans)
    state = jnp.concatenate([before, gathered, after], axis=2)

    for b in range(BLOCKS):
        state = block(state, conv_w[b], depth_k[b], proj_w[b])
        left = halo - 1 - b
        if left > 0:
            n_rows, n_cols = state.shape[1], state.shape[2]
            row = band * rows - left + lax.broadcasted_iota(jnp.int32, (n_rows, n_cols), 0)
            col = side * cols - left + lax.broadcasted_iota(jnp.int32, (n_rows, n_cols), 1)
            inside = (row >= 0) & (row < height) & (col >= 0) & (col < sides * cols)
            state = jnp.where(inside[None, :, :, None], state, jnp.zeros((), state.dtype))

    return lax.all_to_all(state, "tm", 0, 1, tiled=True)


def solution(mesh):
    return jax.shard_map(
        shards,
        mesh=mesh,
        in_specs=(P(("groups", "tm"), None, "width", None), P(), P(), P()),
        out_specs=P(("groups", "tm"), None, "width", None),
        check_vma=False,
    )
```

```python
import jax
import jax.numpy as jnp
from jax import lax
from jax.sharding import PartitionSpec as P

BLOCKS = 2


def conv3x3(x, weight):
    return lax.conv_general_dilated(
        x,
        weight,
        window_strides=(1, 1),
        padding="VALID",
        dimension_numbers=("NHWC", "HWIO", "NHWC"),
        preferred_element_type=jnp.float32,
    )


def block(x, weight, kernel, proj):
    chans = x.shape[-1]
    hidden = jax.nn.silu(conv3x3(x, weight)).astype(jnp.bfloat16)
    frames = hidden.shape[0]
    values = hidden.astype(jnp.float32)
    depth = values * kernel[0]
    for lag in range(1, frames):
        shifted = jnp.pad(values[: frames - lag], ((lag, 0), (0, 0), (0, 0), (0, 0)))
        depth = depth + shifted * kernel[lag]
    depth = depth.astype(jnp.bfloat16)
    mixed = jnp.dot(depth.reshape(-1, chans), proj, preferred_element_type=jnp.float32)
    mixed = mixed.reshape(hidden.shape).astype(jnp.bfloat16)
    inner = x[:, 1:-1, 1:-1, :]
    return (inner.astype(jnp.float32) + mixed.astype(jnp.float32)).astype(jnp.bfloat16)


def shards(video, conv_w, depth_k, proj_w):
    bands = lax.axis_size("tm")
    sides = lax.axis_size("width")
    band = lax.axis_index("tm")
    side = lax.axis_index("width")
    frames, height, cols, chans = video.shape
    rows = height // bands
    halo = BLOCKS

    padded = jnp.pad(video, ((0, 0), (halo, halo), (0, 0), (0, 0)))
    pieces = jnp.stack([padded[:, r * rows : r * rows + rows + 2 * halo] for r in range(bands)])
    gathered = lax.all_to_all(pieces, "tm", 0, 0, tiled=False)
    gathered = gathered.reshape(bands * frames, rows + 2 * halo, cols, chans)

    up = [(i, i + 1) for i in range(sides - 1)]
    down = [(i + 1, i) for i in range(sides - 1)]
    before = lax.ppermute(gathered[:, :, cols - halo :], "width", up)
    after = lax.ppermute(gathered[:, :, :halo], "width", down)

    inner = block(gathered, conv_w[0], depth_k[0], proj_w[0])
    reach = 2 * halo
    rims = jnp.concatenate([before, gathered[:, :, :reach], gathered[:, :, cols - reach :], after], axis=2)
    rims = block(rims, conv_w[0], depth_k[0], proj_w[0])
    state = jnp.concatenate([rims[:, :, :halo], inner, rims[:, :, rims.shape[2] - halo :]], axis=2)

    for b in range(1, BLOCKS):
        left = halo - b
        n_rows, n_cols = state.shape[1], state.shape[2]
        row = band * rows - left + lax.broadcasted_iota(jnp.int32, (n_rows, n_cols), 0)
        col = side * cols - left + lax.broadcasted_iota(jnp.int32, (n_rows, n_cols), 1)
        inside = (row >= 0) & (row < height) & (col >= 0) & (col < sides * cols)
        state = jnp.where(inside[None, :, :, None], state, jnp.zeros((), state.dtype))
        state = block(state, conv_w[b], depth_k[b], proj_w[b])

    return lax.all_to_all(state, "tm", 0, 1, tiled=True)


def solution(mesh):
    return jax.shard_map(
        shards,
        mesh=mesh,
        in_specs=(P(("groups", "tm"), None, "width", None), P(), P(), P()),
        out_specs=P(("groups", "tm"), None, "width", None),
        check_vma=False,
    )
```

```python
import functools

import jax
import jax.numpy as jnp
from jax import lax
from jax.experimental import pallas as pl
from jax.experimental.pallas import tpu as pltpu
from jax.sharding import PartitionSpec as P

BLOCKS = 2
LANES = 16


def block_kernel(x_ref, w_ref, k_ref, p_ref, m_ref, o_ref, *, count, pitch):
    frames, _, chans = x_ref.shape
    total = frames * count

    def window(dy):
        return x_ref[:, dy * pitch : dy * pitch + count, :].reshape(total, chans)

    taps = [None, None, None]
    for dy in range(3):
        piece = window(dy)
        for dx in range(3):
            part = jnp.dot(piece, w_ref[dy, dx], preferred_element_type=jnp.float32)
            taps[dx] = part if taps[dx] is None else taps[dx] + part
    conv = taps[0] + pltpu.roll(taps[1], total - 1, 0) + pltpu.roll(taps[2], total - 2, 0)
    hidden = (conv / (1.0 + jnp.exp(-conv))).astype(jnp.bfloat16)

    values = hidden.astype(jnp.float32).reshape(frames, count, chans)
    kernel = k_ref[...]
    depth = []
    for t in range(frames):
        acc = values[t] * kernel[0:1]
        for lag in range(1, t + 1):
            acc = acc + values[t - lag] * kernel[lag : lag + 1]
        depth.append(acc.astype(jnp.bfloat16))
    depth = jnp.stack(depth).reshape(total, chans)

    mixed = jnp.dot(depth, p_ref[...], preferred_element_type=jnp.float32).astype(jnp.bfloat16)
    center = pltpu.roll(window(1).astype(jnp.float32), total - 1, 0)
    state = (center + mixed.astype(jnp.float32)).astype(jnp.bfloat16).reshape(frames, count, chans)
    o_ref[...] = jnp.where(m_ref[...][None] > 0, state, jnp.zeros((), state.dtype))


def block(x, weight, kernel, proj, mask, pitch):
    frames, length, chans = x.shape
    count = length - 2 * pitch
    flops = 2 * frames * count * chans * chans * 10
    vmem = pltpu.VMEM
    return pl.pallas_call(
        functools.partial(block_kernel, count=count, pitch=pitch),
        out_shape=jax.ShapeDtypeStruct((frames, count, chans), x.dtype),
        in_specs=[pl.BlockSpec(memory_space=vmem)] * 5,
        out_specs=pl.BlockSpec(memory_space=vmem),
        compiler_params=pltpu.CompilerParams(vmem_limit_bytes=48 * 1024 * 1024),
        cost_estimate=pl.CostEstimate(
            flops=flops,
            transcendentals=frames * count * chans,
            bytes_accessed=2 * frames * (length + count) * chans + 2 * 10 * chans * chans,
        ),
    )(x, weight, kernel, proj, mask)


def shards(video, conv_w, depth_k, proj_w):
    bands = lax.axis_size("tm")
    sides = lax.axis_size("width")
    band = lax.axis_index("tm")
    side = lax.axis_index("width")
    frames, height, cols, chans = video.shape
    rows = height // bands
    halo = BLOCKS
    pitch = -(-(cols + 2 * halo) // LANES) * LANES

    padded = jnp.pad(video, ((0, 0), (halo, halo), (0, 0), (0, 0)))
    pieces = jnp.stack([padded[:, r * rows : r * rows + rows + 2 * halo] for r in range(bands)])
    gathered = lax.all_to_all(pieces, "tm", 0, 0, tiled=False)
    gathered = gathered.reshape(bands * frames, rows + 2 * halo, cols, chans)

    up = [(i, i + 1) for i in range(sides - 1)]
    down = [(i + 1, i) for i in range(sides - 1)]
    before = lax.ppermute(gathered[:, :, cols - halo :], "width", up)
    after = lax.ppermute(gathered[:, :, :halo], "width", down)
    spare = jnp.zeros(gathered.shape[:2] + (pitch - cols - 2 * halo, chans), gathered.dtype)
    state = jnp.concatenate([before, gathered, after, spare], axis=2)
    state = state.reshape(state.shape[0], -1, chans)

    for b in range(BLOCKS):
        left = halo - 1 - b
        n_rows = rows + 2 * left
        row = band * rows - left + lax.broadcasted_iota(jnp.int32, (n_rows, pitch), 0)
        col = side * cols - left + lax.broadcasted_iota(jnp.int32, (n_rows, pitch), 1)
        inside = (row >= 0) & (row < height) & (col >= 0) & (col < sides * cols)
        inside = inside & (lax.broadcasted_iota(jnp.int32, (n_rows, pitch), 1) < cols + 2 * left)
        mask = jnp.broadcast_to(inside.reshape(-1, 1), (n_rows * pitch, chans)).astype(jnp.float32)
        state = block(state, conv_w[b], depth_k[b], proj_w[b], mask, pitch)

    state = state.reshape(state.shape[0], rows, pitch, chans)[:, :, :cols]
    return lax.all_to_all(state, "tm", 0, 1, tiled=True)


def solution(mesh):
    return jax.shard_map(
        shards,
        mesh=mesh,
        in_specs=(P(("groups", "tm"), None, "width", None), P(), P(), P()),
        out_specs=P(("groups", "tm"), None, "width", None),
        check_vma=False,
    )
```

```python
import functools

import jax
import jax.numpy as jnp
from jax import lax
from jax.experimental import pallas as pl
from jax.experimental.pallas import tpu as pltpu
from jax.sharding import PartitionSpec as P

BLOCKS = 2
LANES = 16


def block_kernel(x_ref, w_ref, k_ref, p_ref, m_ref, o_ref, *, count, pitch):
    frames, _, chans = x_ref.shape
    total = frames * count

    def window(dy):
        return x_ref[:, dy * pitch : dy * pitch + count, :].reshape(total, chans)

    taps = [None, None, None]
    for dy in range(3):
        piece = window(dy)
        for dx in range(3):
            part = jnp.dot(piece, w_ref[dy, dx], preferred_element_type=jnp.float32)
            taps[dx] = part if taps[dx] is None else taps[dx] + part
    conv = taps[0] + pltpu.roll(taps[1], total - 1, 0) + pltpu.roll(taps[2], total - 2, 0)
    hidden = (conv / (1.0 + jnp.exp(-conv))).astype(jnp.bfloat16)

    values = hidden.astype(jnp.float32).reshape(frames, count, chans)
    kernel = k_ref[...]
    depth = []
    for t in range(frames):
        acc = values[t] * kernel[0:1]
        for lag in range(1, t + 1):
            acc = acc + values[t - lag] * kernel[lag : lag + 1]
        depth.append(acc.astype(jnp.bfloat16))
    depth = jnp.stack(depth).reshape(total, chans)

    mixed = jnp.dot(depth, p_ref[...], preferred_element_type=jnp.float32).astype(jnp.bfloat16)
    center = pltpu.roll(window(1).astype(jnp.float32), total - 1, 0)
    state = (center + mixed.astype(jnp.float32)).astype(jnp.bfloat16).reshape(frames, count, chans)
    o_ref[...] = jnp.where(m_ref[...][None] > 0, state, jnp.zeros((), state.dtype))


def block(x, weight, kernel, proj, mask, pitch):
    frames, length, chans = x.shape
    count = length - 2 * pitch
    flops = 2 * frames * count * chans * chans * 10
    vmem = pltpu.VMEM
    return pl.pallas_call(
        functools.partial(block_kernel, count=count, pitch=pitch),
        out_shape=jax.ShapeDtypeStruct((frames, count, chans), x.dtype),
        in_specs=[pl.BlockSpec(memory_space=vmem)] * 5,
        out_specs=pl.BlockSpec(memory_space=vmem),
        compiler_params=pltpu.CompilerParams(vmem_limit_bytes=48 * 1024 * 1024),
        cost_estimate=pl.CostEstimate(
            flops=flops,
            transcendentals=frames * count * chans,
            bytes_accessed=2 * frames * (length + count) * chans + 2 * 10 * chans * chans,
        ),
    )(x, weight, kernel, proj, mask)


def shards(video, conv_w, depth_k, proj_w):
    bands = lax.axis_size("tm")
    sides = lax.axis_size("width")
    band = lax.axis_index("tm")
    side = lax.axis_index("width")
    frames, height, cols, chans = video.shape
    rows = height // bands
    halo = BLOCKS
    pitch = -(-(cols + 2 * halo) // LANES) * LANES

    padded = jnp.pad(video, ((0, 0), (halo, halo), (0, 0), (0, 0)))
    pieces = jnp.stack([padded[:, r * rows : r * rows + rows + 2 * halo] for r in range(bands)])
    received = lax.all_to_all(pieces, "tm", 0, 0, tiled=False)

    up = [(i, i + 1) for i in range(sides - 1)]
    down = [(i + 1, i) for i in range(sides - 1)]
    edge = (bands * frames, rows + 2 * halo, halo, chans)
    before = lax.ppermute(received[:, :, :, cols - halo :], "width", up).reshape(edge)
    after = lax.ppermute(received[:, :, :, :halo], "width", down).reshape(edge)
    gathered = received.reshape(bands * frames, rows + 2 * halo, cols, chans)
    spare = jnp.zeros(gathered.shape[:2] + (pitch - cols - 2 * halo, chans), gathered.dtype)
    state = jnp.concatenate([before, gathered, after, spare], axis=2)
    state = state.reshape(state.shape[0], -1, chans)

    for b in range(BLOCKS):
        left = halo - 1 - b
        n_rows = rows + 2 * left
        row = band * rows - left + lax.broadcasted_iota(jnp.int32, (n_rows, pitch), 0)
        col = side * cols - left + lax.broadcasted_iota(jnp.int32, (n_rows, pitch), 1)
        inside = (row >= 0) & (row < height) & (col >= 0) & (col < sides * cols)
        inside = inside & (lax.broadcasted_iota(jnp.int32, (n_rows, pitch), 1) < cols + 2 * left)
        mask = jnp.broadcast_to(inside.reshape(-1, 1), (n_rows * pitch, chans)).astype(jnp.float32)
        state = block(state, conv_w[b], depth_k[b], proj_w[b], mask, pitch)

    state = state.reshape(state.shape[0], rows, pitch, chans)[:, :, :cols]
    return lax.all_to_all(state, "tm", 0, 1, tiled=True)


def solution(mesh):
    return jax.shard_map(
        shards,
        mesh=mesh,
        in_specs=(P(("groups", "tm"), None, "width", None), P(), P(), P()),
        out_specs=P(("groups", "tm"), None, "width", None),
        check_vma=False,
    )
```

```python
import functools

import jax
import jax.numpy as jnp
from jax import lax
from jax.experimental import pallas as pl
from jax.experimental.pallas import tpu as pltpu
from jax.sharding import PartitionSpec as P

BLOCKS = 2
LANES = 16


def block_kernel(x_ref, w_ref, k_ref, p_ref, m_ref, o_ref, *, count, pitch):
    frames, _, chans = x_ref.shape
    total = frames * count

    def window(dy):
        return x_ref[:, dy * pitch : dy * pitch + count, :].reshape(total, chans)

    taps = [None, None, None]
    for dy in range(3):
        piece = window(dy)
        for dx in range(3):
            part = jnp.dot(piece, w_ref[dy, dx], preferred_element_type=jnp.float32)
            taps[dx] = part if taps[dx] is None else taps[dx] + part
    conv = taps[0] + pltpu.roll(taps[1], total - 1, 0) + pltpu.roll(taps[2], total - 2, 0)
    hidden = (conv / (1.0 + jnp.exp(-conv))).astype(jnp.bfloat16)

    values = hidden.astype(jnp.float32).reshape(frames, count, chans)
    kernel = k_ref[...]
    depth = []
    for t in range(frames):
        acc = values[t] * kernel[0:1]
        for lag in range(1, t + 1):
            acc = acc + values[t - lag] * kernel[lag : lag + 1]
        depth.append(acc.astype(jnp.bfloat16))
    depth = jnp.stack(depth).reshape(total, chans)

    mixed = jnp.dot(depth, p_ref[...], preferred_element_type=jnp.float32).astype(jnp.bfloat16)
    center = pltpu.roll(window(1).astype(jnp.float32), total - 1, 0)
    state = (center + mixed.astype(jnp.float32)).astype(jnp.bfloat16).reshape(frames, count, chans)
    o_ref[...] = jnp.where(m_ref[...][None] > 0, state, jnp.zeros((), state.dtype))


def block(x, weight, kernel, proj, mask, pitch):
    frames, length, chans = x.shape
    count = length - 2 * pitch
    flops = 2 * frames * count * chans * chans * 10
    vmem = pltpu.VMEM
    return pl.pallas_call(
        functools.partial(block_kernel, count=count, pitch=pitch),
        out_shape=jax.ShapeDtypeStruct((frames, count, chans), x.dtype),
        in_specs=[pl.BlockSpec(memory_space=vmem)] * 5,
        out_specs=pl.BlockSpec(memory_space=vmem),
        compiler_params=pltpu.CompilerParams(vmem_limit_bytes=48 * 1024 * 1024),
        cost_estimate=pl.CostEstimate(
            flops=flops,
            transcendentals=frames * count * chans,
            bytes_accessed=2 * frames * (length + count) * chans + 2 * 10 * chans * chans,
        ),
    )(x, weight, kernel, proj, mask)


def shards(video, conv_w, depth_k, proj_w):
    bands = lax.axis_size("tm")
    sides = lax.axis_size("width")
    band = lax.axis_index("tm")
    side = lax.axis_index("width")
    frames, height, cols, chans = video.shape
    rows = height // bands
    halo = BLOCKS
    pitch = -(-(cols + 2 * halo) // LANES) * LANES

    padded = jnp.pad(video, ((0, 0), (halo, halo), (0, 0), (0, 0)))
    pieces = jnp.stack([padded[:, r * rows : r * rows + rows + 2 * halo] for r in range(bands)])
    received = lax.all_to_all(pieces, "tm", 0, 0, tiled=False)

    up = [(i, i + 1) for i in range(sides - 1)]
    down = [(i + 1, i) for i in range(sides - 1)]
    before = lax.ppermute(received[:, :, :, cols - halo :], "width", up)
    after = lax.ppermute(received[:, :, :, :halo], "width", down)
    spare = jnp.zeros(received.shape[:3] + (pitch - cols - 2 * halo, chans), received.dtype)
    state = jnp.concatenate([before, received, after, spare], axis=3)
    state = state.reshape(bands * frames, -1, chans)

    for b in range(BLOCKS):
        left = halo - 1 - b
        n_rows = rows + 2 * left
        row = band * rows - left + lax.broadcasted_iota(jnp.int32, (n_rows, pitch), 0)
        col = side * cols - left + lax.broadcasted_iota(jnp.int32, (n_rows, pitch), 1)
        inside = (row >= 0) & (row < height) & (col >= 0) & (col < sides * cols)
        inside = inside & (lax.broadcasted_iota(jnp.int32, (n_rows, pitch), 1) < cols + 2 * left)
        mask = jnp.broadcast_to(inside.reshape(-1, 1), (n_rows * pitch, chans)).astype(jnp.float32)
        state = block(state, conv_w[b], depth_k[b], proj_w[b], mask, pitch)

    state = state.reshape(state.shape[0], rows, pitch, chans)[:, :, :cols]
    return lax.all_to_all(state, "tm", 0, 1, tiled=True)


def solution(mesh):
    return jax.shard_map(
        shards,
        mesh=mesh,
        in_specs=(P(("groups", "tm"), None, "width", None), P(), P(), P()),
        out_specs=P(("groups", "tm"), None, "width", None),
        check_vma=False,
    )
```

```python
import functools

import jax
import jax.numpy as jnp
from jax import lax
from jax.experimental import pallas as pl
from jax.experimental.pallas import tpu as pltpu
from jax.sharding import PartitionSpec as P

BLOCKS = 2
LANES = 16


def block_kernel(x_ref, w_ref, k_ref, p_ref, m_ref, o_ref, *, count, pitch):
    frames, _, chans = x_ref.shape
    total = frames * count

    def window(dy):
        return x_ref[:, dy * pitch : dy * pitch + count, :].reshape(total, chans)

    taps = [None, None, None]
    for dy in range(3):
        piece = window(dy)
        for dx in range(3):
            part = jnp.dot(piece, w_ref[dy, dx], preferred_element_type=jnp.float32)
            taps[dx] = part if taps[dx] is None else taps[dx] + part
    conv = taps[0] + pltpu.roll(taps[1], total - 1, 0) + pltpu.roll(taps[2], total - 2, 0)
    hidden = (conv / (1.0 + jnp.exp(-conv))).astype(jnp.bfloat16)

    values = hidden.astype(jnp.float32).reshape(frames, count, chans)
    kernel = k_ref[...]
    depth = []
    for t in range(frames):
        acc = values[t] * kernel[0:1]
        for lag in range(1, t + 1):
            acc = acc + values[t - lag] * kernel[lag : lag + 1]
        depth.append(acc.astype(jnp.bfloat16))
    depth = jnp.stack(depth).reshape(total, chans)

    mixed = jnp.dot(depth, p_ref[...], preferred_element_type=jnp.float32).astype(jnp.bfloat16)
    center = pltpu.roll(window(1).astype(jnp.float32), total - 1, 0)
    state = (center + mixed.astype(jnp.float32)).astype(jnp.bfloat16).reshape(frames, count, chans)
    o_ref[...] = jnp.where(m_ref[...][None] > 0, state, jnp.zeros((), state.dtype))


def block(x, weight, kernel, proj, mask, pitch):
    frames, length, chans = x.shape
    count = length - 2 * pitch
    flops = 2 * frames * count * chans * chans * 10
    vmem = pltpu.VMEM
    return pl.pallas_call(
        functools.partial(block_kernel, count=count, pitch=pitch),
        out_shape=jax.ShapeDtypeStruct((frames, count, chans), x.dtype),
        in_specs=[pl.BlockSpec(memory_space=vmem)] * 5,
        out_specs=pl.BlockSpec(memory_space=vmem),
        compiler_params=pltpu.CompilerParams(vmem_limit_bytes=48 * 1024 * 1024),
        cost_estimate=pl.CostEstimate(
            flops=flops,
            transcendentals=frames * count * chans,
            bytes_accessed=2 * frames * (length + count) * chans + 2 * 10 * chans * chans,
        ),
    )(x, weight, kernel, proj, mask)


def shards(video, conv_w, depth_k, proj_w):
    bands = lax.axis_size("tm")
    sides = lax.axis_size("width")
    band = lax.axis_index("tm")
    side = lax.axis_index("width")
    frames, height, cols, chans = video.shape
    rows = height // bands
    halo = BLOCKS
    pitch = -(-(cols + 2 * halo) // LANES) * LANES

    padded = jnp.pad(video, ((0, 0), (halo, halo), (0, 0), (0, 0)))
    pieces = jnp.stack([padded[:, r * rows : r * rows + rows + 2 * halo] for r in range(bands)])
    received = lax.all_to_all(pieces, "tm", 0, 0, tiled=False)

    lead = received[:, :, :, :halo]
    tail = received[:, :, :, cols - halo :]
    target = lax.broadcasted_iota(jnp.int32, (sides,) + (1,) * lead.ndim, 0)
    zero = jnp.zeros((), lead.dtype)
    edges = jnp.where(target == side + 1, tail[None], jnp.where(target == side - 1, lead[None], zero))
    edges = lax.all_to_all(edges, "width", 0, 0, tiled=False)
    before = lax.dynamic_index_in_dim(edges, jnp.maximum(side - 1, 0), 0, keepdims=False)
    after = lax.dynamic_index_in_dim(edges, jnp.minimum(side + 1, sides - 1), 0, keepdims=False)
    before = jnp.where(side > 0, before, zero)
    after = jnp.where(side < sides - 1, after, zero)
    spare = jnp.zeros(received.shape[:3] + (pitch - cols - 2 * halo, chans), received.dtype)
    state = jnp.concatenate([before, received, after, spare], axis=3)
    state = state.reshape(bands * frames, -1, chans)

    for b in range(BLOCKS):
        left = halo - 1 - b
        n_rows = rows + 2 * left
        row = band * rows - left + lax.broadcasted_iota(jnp.int32, (n_rows, pitch), 0)
        col = side * cols - left + lax.broadcasted_iota(jnp.int32, (n_rows, pitch), 1)
        inside = (row >= 0) & (row < height) & (col >= 0) & (col < sides * cols)
        inside = inside & (lax.broadcasted_iota(jnp.int32, (n_rows, pitch), 1) < cols + 2 * left)
        mask = jnp.broadcast_to(inside.reshape(-1, 1), (n_rows * pitch, chans)).astype(jnp.float32)
        state = block(state, conv_w[b], depth_k[b], proj_w[b], mask, pitch)

    state = state.reshape(state.shape[0], rows, pitch, chans)[:, :, :cols]
    return lax.all_to_all(state, "tm", 0, 1, tiled=True)


def solution(mesh):
    return jax.shard_map(
        shards,
        mesh=mesh,
        in_specs=(P(("groups", "tm"), None, "width", None), P(), P(), P()),
        out_specs=P(("groups", "tm"), None, "width", None),
        check_vma=False,
    )
```

```python
import functools

import jax
import jax.numpy as jnp
from jax import lax
from jax.experimental import pallas as pl
from jax.experimental.pallas import tpu as pltpu
from jax.sharding import PartitionSpec as P

BLOCKS = 2
LANES = 16


def block_kernel(x_ref, w_ref, k_ref, p_ref, m_ref, o_ref, *, count, pitch):
    frames, _, chans = x_ref.shape
    total = frames * count

    def window(dy):
        return x_ref[:, dy * pitch : dy * pitch + count, :].reshape(total, chans)

    taps = [None, None, None]
    for dy in range(3):
        piece = window(dy)
        for dx in range(3):
            part = jnp.dot(piece, w_ref[dy, dx], preferred_element_type=jnp.float32)
            taps[dx] = part if taps[dx] is None else taps[dx] + part
    conv = taps[0] + pltpu.roll(taps[1], total - 1, 0) + pltpu.roll(taps[2], total - 2, 0)
    hidden = (conv / (1.0 + jnp.exp(-conv))).astype(jnp.bfloat16)

    values = hidden.astype(jnp.float32).reshape(frames, count, chans)
    kernel = k_ref[...]
    depth = []
    for t in range(frames):
        acc = values[t] * kernel[0:1]
        for lag in range(1, t + 1):
            acc = acc + values[t - lag] * kernel[lag : lag + 1]
        depth.append(acc.astype(jnp.bfloat16))
    depth = jnp.stack(depth).reshape(total, chans)

    mixed = jnp.dot(depth, p_ref[...], preferred_element_type=jnp.float32).astype(jnp.bfloat16)
    center = pltpu.roll(window(1).astype(jnp.float32), total - 1, 0)
    state = (center + mixed.astype(jnp.float32)).astype(jnp.bfloat16).reshape(frames, count, chans)
    o_ref[...] = jnp.where(m_ref[...][None] > 0, state, jnp.zeros((), state.dtype))


def block(x, weight, kernel, proj, mask, pitch):
    frames, length, chans = x.shape
    count = length - 2 * pitch
    flops = 2 * frames * count * chans * chans * 10
    vmem = pltpu.VMEM
    return pl.pallas_call(
        functools.partial(block_kernel, count=count, pitch=pitch),
        out_shape=jax.ShapeDtypeStruct((frames, count, chans), x.dtype),
        in_specs=[pl.BlockSpec(memory_space=vmem)] * 5,
        out_specs=pl.BlockSpec(memory_space=vmem),
        compiler_params=pltpu.CompilerParams(vmem_limit_bytes=48 * 1024 * 1024),
        cost_estimate=pl.CostEstimate(
            flops=flops,
            transcendentals=frames * count * chans,
            bytes_accessed=2 * frames * (length + count) * chans + 2 * 10 * chans * chans,
        ),
    )(x, weight, kernel, proj, mask)


def shards(video, conv_w, depth_k, proj_w):
    bands = lax.axis_size("tm")
    sides = lax.axis_size("width")
    band = lax.axis_index("tm")
    side = lax.axis_index("width")
    frames, height, cols, chans = video.shape
    rows = height // bands
    halo = BLOCKS
    pitch = -(-(cols + 2 * halo) // LANES) * LANES

    spans = -(-(rows + 2 * halo) // rows)
    padded = jnp.pad(video, ((0, 0), (halo, (bands + spans - 1) * rows - height - halo), (0, 0), (0, 0)))
    windows = [padded[:, j * rows : (j + bands) * rows].reshape(frames, bands, rows, cols, chans) for j in range(spans)]
    pieces = jnp.concatenate(windows, axis=2)[:, :, : rows + 2 * halo]
    pieces = jnp.transpose(pieces, (1, 0, 2, 3, 4))
    received = lax.all_to_all(pieces, "tm", 0, 0, tiled=False)

    up = [(i, i + 1) for i in range(sides - 1)]
    down = [(i + 1, i) for i in range(sides - 1)]
    before = lax.ppermute(received[:, :, :, cols - halo :], "width", up)
    after = lax.ppermute(received[:, :, :, :halo], "width", down)
    spare = jnp.zeros(received.shape[:3] + (pitch - cols - 2 * halo, chans), received.dtype)
    state = jnp.concatenate([before, received, after, spare], axis=3)
    state = state.reshape(bands * frames, -1, chans)

    for b in range(BLOCKS):
        left = halo - 1 - b
        n_rows = rows + 2 * left
        row = band * rows - left + lax.broadcasted_iota(jnp.int32, (n_rows, pitch), 0)
        col = side * cols - left + lax.broadcasted_iota(jnp.int32, (n_rows, pitch), 1)
        inside = (row >= 0) & (row < height) & (col >= 0) & (col < sides * cols)
        inside = inside & (lax.broadcasted_iota(jnp.int32, (n_rows, pitch), 1) < cols + 2 * left)
        mask = jnp.broadcast_to(inside.reshape(-1, 1), (n_rows * pitch, chans)).astype(jnp.float32)
        state = block(state, conv_w[b], depth_k[b], proj_w[b], mask, pitch)

    state = state.reshape(state.shape[0], rows, pitch, chans)[:, :, :cols]
    return lax.all_to_all(state, "tm", 0, 1, tiled=True)


def solution(mesh):
    return jax.shard_map(
        shards,
        mesh=mesh,
        in_specs=(P(("groups", "tm"), None, "width", None), P(), P(), P()),
        out_specs=P(("groups", "tm"), None, "width", None),
        check_vma=False,
    )
```

```python
import functools

import jax
import jax.numpy as jnp
from jax import lax
from jax.experimental import pallas as pl
from jax.experimental.pallas import tpu as pltpu
from jax.sharding import PartitionSpec as P

BLOCKS = 2
LANES = 16


def run_block(x_ref, w_ref, k_ref, p_ref, b, count, pitch):
    frames, _, chans = x_ref.shape
    total = frames * count

    def window(dy):
        return x_ref[:, dy * pitch : dy * pitch + count, :].reshape(total, chans)

    taps = [None, None, None]
    for dy in range(3):
        piece = window(dy)
        for dx in range(3):
            part = jnp.dot(piece, w_ref[b, dy, dx], preferred_element_type=jnp.float32)
            taps[dx] = part if taps[dx] is None else taps[dx] + part
    conv = taps[0] + pltpu.roll(taps[1], total - 1, 0) + pltpu.roll(taps[2], total - 2, 0)
    hidden = (conv / (1.0 + jnp.exp(-conv))).astype(jnp.bfloat16)

    values = hidden.astype(jnp.float32).reshape(frames, count, chans)
    kernel = k_ref[b]
    depth = []
    for t in range(frames):
        acc = values[t] * kernel[0:1]
        for lag in range(1, t + 1):
            acc = acc + values[t - lag] * kernel[lag : lag + 1]
        depth.append(acc.astype(jnp.bfloat16))
    depth = jnp.stack(depth).reshape(total, chans)

    mixed = jnp.dot(depth, p_ref[b], preferred_element_type=jnp.float32).astype(jnp.bfloat16)
    center = pltpu.roll(window(1).astype(jnp.float32), total - 1, 0)
    return (center + mixed.astype(jnp.float32)).astype(jnp.bfloat16).reshape(frames, count, chans)


def blocks_kernel(x_ref, w_ref, k_ref, p_ref, *rest, pitch):
    masks = rest[: BLOCKS - 1]
    o_ref = rest[BLOCKS - 1]
    held = rest[BLOCKS:]
    source = x_ref
    for b in range(BLOCKS):
        target = o_ref if b == BLOCKS - 1 else held[b]
        count = target.shape[1]
        state = run_block(source, w_ref, k_ref, p_ref, b, count, pitch)
        if b < BLOCKS - 1:
            state = jnp.where(masks[b][...][None] > 0, state, jnp.zeros((), state.dtype))
        target[...] = state
        source = target


def all_blocks(x, conv_w, depth_k, proj_w, masks, pitch):
    frames, length, chans = x.shape
    counts = [length - 2 * pitch * (b + 1) for b in range(BLOCKS)]
    flops = sum(2 * frames * n * chans * chans * 10 for n in counts)
    vmem = pltpu.VMEM
    return pl.pallas_call(
        functools.partial(blocks_kernel, pitch=pitch),
        out_shape=jax.ShapeDtypeStruct((frames, counts[-1], chans), x.dtype),
        in_specs=[pl.BlockSpec(memory_space=vmem)] * (4 + len(masks)),
        out_specs=pl.BlockSpec(memory_space=vmem),
        scratch_shapes=[pltpu.VMEM((frames, n, chans), x.dtype) for n in counts[:-1]],
        compiler_params=pltpu.CompilerParams(vmem_limit_bytes=48 * 1024 * 1024),
        cost_estimate=pl.CostEstimate(
            flops=flops,
            transcendentals=frames * sum(counts) * chans,
            bytes_accessed=2 * frames * (length + counts[-1]) * chans + 2 * BLOCKS * 10 * chans * chans,
        ),
    )(x, conv_w, depth_k, proj_w, *masks)


def shards(video, conv_w, depth_k, proj_w):
    bands = lax.axis_size("tm")
    sides = lax.axis_size("width")
    band = lax.axis_index("tm")
    side = lax.axis_index("width")
    frames, height, cols, chans = video.shape
    rows = height // bands
    halo = BLOCKS
    pitch = -(-(cols + 2 * halo) // LANES) * LANES

    padded = jnp.pad(video, ((0, 0), (halo, halo), (0, 0), (0, 0)))
    pieces = jnp.stack([padded[:, r * rows : r * rows + rows + 2 * halo] for r in range(bands)])
    received = lax.all_to_all(pieces, "tm", 0, 0, tiled=False)

    up = [(i, i + 1) for i in range(sides - 1)]
    down = [(i + 1, i) for i in range(sides - 1)]
    before = lax.ppermute(received[:, :, :, cols - halo :], "width", up)
    after = lax.ppermute(received[:, :, :, :halo], "width", down)
    spare = jnp.zeros(received.shape[:3] + (pitch - cols - 2 * halo, chans), received.dtype)
    state = jnp.concatenate([before, received, after, spare], axis=3)
    state = state.reshape(bands * frames, -1, chans)

    masks = []
    for b in range(BLOCKS - 1):
        left = halo - 1 - b
        n_rows = rows + 2 * left
        row = band * rows - left + lax.broadcasted_iota(jnp.int32, (n_rows, pitch), 0)
        col = side * cols - left + lax.broadcasted_iota(jnp.int32, (n_rows, pitch), 1)
        inside = (row >= 0) & (row < height) & (col >= 0) & (col < sides * cols)
        inside = inside & (lax.broadcasted_iota(jnp.int32, (n_rows, pitch), 1) < cols + 2 * left)
        masks.append(jnp.broadcast_to(inside.reshape(-1, 1), (n_rows * pitch, chans)).astype(jnp.float32))
    state = all_blocks(state, conv_w, depth_k, proj_w, masks, pitch)

    state = state.reshape(state.shape[0], rows, pitch, chans)[:, :, :cols]
    return lax.all_to_all(state, "tm", 0, 1, tiled=True)


def solution(mesh):
    return jax.shard_map(
        shards,
        mesh=mesh,
        in_specs=(P(("groups", "tm"), None, "width", None), P(), P(), P()),
        out_specs=P(("groups", "tm"), None, "width", None),
        check_vma=False,
    )
```

```python
import functools

import jax
import jax.numpy as jnp
from jax import lax
from jax.experimental import pallas as pl
from jax.experimental.pallas import tpu as pltpu
from jax.sharding import PartitionSpec as P

BLOCKS = 2
LANES = 16


def block_kernel(x_ref, w_ref, k_ref, p_ref, m_ref, o_ref, *, count, pitch):
    frames, _, chans = x_ref.shape
    total = frames * count

    def window(dy):
        return x_ref[:, dy * pitch : dy * pitch + count, :].reshape(total, chans)

    taps = [None, None, None]
    for dy in range(3):
        piece = window(dy)
        for dx in range(3):
            part = jnp.dot(piece, w_ref[dy, dx], preferred_element_type=jnp.float32)
            taps[dx] = part if taps[dx] is None else taps[dx] + part
    conv = taps[0] + pltpu.roll(taps[1], total - 1, 0) + pltpu.roll(taps[2], total - 2, 0)
    hidden = (conv / (1.0 + jnp.exp(-conv))).astype(jnp.bfloat16)

    values = hidden.astype(jnp.float32).reshape(frames, count, chans)
    kernel = k_ref[...]
    depth = []
    for t in range(frames):
        acc = values[t] * kernel[0:1]
        for lag in range(1, t + 1):
            acc = acc + values[t - lag] * kernel[lag : lag + 1]
        depth.append(acc.astype(jnp.bfloat16))
    depth = jnp.stack(depth).reshape(total, chans)

    mixed = jnp.dot(depth, p_ref[...], preferred_element_type=jnp.float32).astype(jnp.bfloat16)
    center = pltpu.roll(window(1).astype(jnp.float32), total - 1, 0)
    state = (center + mixed.astype(jnp.float32)).astype(jnp.bfloat16).reshape(frames, count, chans)
    o_ref[...] = jnp.where(m_ref[...][None] > 0, state, jnp.zeros((), state.dtype))


def block(x, weight, kernel, proj, mask, pitch):
    frames, length, chans = x.shape
    count = length - 2 * pitch
    flops = 2 * frames * count * chans * chans * 10
    vmem = pltpu.VMEM
    return pl.pallas_call(
        functools.partial(block_kernel, count=count, pitch=pitch),
        out_shape=jax.ShapeDtypeStruct((frames, count, chans), x.dtype),
        in_specs=[pl.BlockSpec(memory_space=vmem)] * 5,
        out_specs=pl.BlockSpec(memory_space=vmem),
        compiler_params=pltpu.CompilerParams(vmem_limit_bytes=48 * 1024 * 1024),
        cost_estimate=pl.CostEstimate(
            flops=flops,
            transcendentals=frames * count * chans,
            bytes_accessed=2 * frames * (length + count) * chans + 2 * 10 * chans * chans,
        ),
    )(x, weight, kernel, proj, mask)


def bands_kernel(v_ref, o_ref, zero_ref, sems, *, rows, halo):
    height = v_ref.shape[0]
    zero_ref[...] = jnp.zeros(zero_ref.shape, zero_ref.dtype)
    copies = []
    for r in range(o_ref.shape[0]):
        lo = r * rows - halo
        hi = lo + rows + 2 * halo
        first, last = max(lo, 0), min(hi, height)
        parts = [(v_ref.at[first:last], o_ref.at[r, first - lo : last - lo])]
        if first > lo:
            parts.append((zero_ref.at[: first - lo], o_ref.at[r, : first - lo]))
        if last < hi:
            parts.append((zero_ref.at[: hi - last], o_ref.at[r, last - lo :]))
        for src, dst in parts:
            copy = pltpu.make_async_copy(src, dst, sems.at[len(copies)])
            copy.start()
            copies.append(copy)
    for copy in copies:
        copy.wait()


def row_bands(video_t, bands, rows, halo):
    height, cols, frames, chans = video_t.shape
    count = bands + 2 * sum(1 for r in range(bands) for edge in (r * rows - halo < 0, r * rows + rows + halo > height) if edge)
    return pl.pallas_call(
        functools.partial(bands_kernel, rows=rows, halo=halo),
        out_shape=jax.ShapeDtypeStruct((bands, rows + 2 * halo, cols, frames, chans), video_t.dtype),
        in_specs=[pl.BlockSpec(memory_space=pl.ANY)],
        out_specs=pl.BlockSpec(memory_space=pl.ANY),
        scratch_shapes=[pltpu.VMEM((halo, cols, frames, chans), video_t.dtype), pltpu.SemaphoreType.DMA((count,))],
    )(video_t)


def shards(video, conv_w, depth_k, proj_w):
    bands = lax.axis_size("tm")
    sides = lax.axis_size("width")
    band = lax.axis_index("tm")
    side = lax.axis_index("width")
    frames, height, cols, chans = video.shape
    rows = height // bands
    halo = BLOCKS
    pitch = -(-(cols + 2 * halo) // LANES) * LANES

    pieces = row_bands(jnp.transpose(video, (1, 2, 0, 3)), bands, rows, halo)
    received = lax.all_to_all(pieces, "tm", 0, 0, tiled=False)
    received = jnp.transpose(received, (0, 3, 1, 2, 4))

    up = [(i, i + 1) for i in range(sides - 1)]
    down = [(i + 1, i) for i in range(sides - 1)]
    before = lax.ppermute(received[:, :, :, cols - halo :], "width", up)
    after = lax.ppermute(received[:, :, :, :halo], "width", down)
    spare = jnp.zeros(received.shape[:3] + (pitch - cols - 2 * halo, chans), received.dtype)
    state = jnp.concatenate([before, received, after, spare], axis=3)
    state = state.reshape(bands * frames, -1, chans)

    for b in range(BLOCKS):
        left = halo - 1 - b
        n_rows = rows + 2 * left
        row = band * rows - left + lax.broadcasted_iota(jnp.int32, (n_rows, pitch), 0)
        col = side * cols - left + lax.broadcasted_iota(jnp.int32, (n_rows, pitch), 1)
        inside = (row >= 0) & (row < height) & (col >= 0) & (col < sides * cols)
        inside = inside & (lax.broadcasted_iota(jnp.int32, (n_rows, pitch), 1) < cols + 2 * left)
        mask = jnp.broadcast_to(inside.reshape(-1, 1), (n_rows * pitch, chans)).astype(jnp.float32)
        state = block(state, conv_w[b], depth_k[b], proj_w[b], mask, pitch)

    state = state.reshape(state.shape[0], rows, pitch, chans)[:, :, :cols]
    return lax.all_to_all(state, "tm", 0, 1, tiled=True)


def solution(mesh):
    return jax.shard_map(
        shards,
        mesh=mesh,
        in_specs=(P(("groups", "tm"), None, "width", None), P(), P(), P()),
        out_specs=P(("groups", "tm"), None, "width", None),
        check_vma=False,
    )
```

```python
import functools

import jax
import jax.numpy as jnp
from jax import lax
from jax.experimental import pallas as pl
from jax.experimental.pallas import tpu as pltpu
from jax.sharding import PartitionSpec as P

BLOCKS = 2
LANES = 16


def block_kernel(x_ref, w_ref, k_ref, p_ref, m_ref, o_ref, *, count, pitch):
    frames, _, chans = x_ref.shape
    total = frames * count

    def window(dy):
        return x_ref[:, dy * pitch : dy * pitch + count, :].reshape(total, chans)

    pieces = jnp.concatenate([window(dy) for dy in range(3)], axis=1)
    taps = []
    for dx in range(3):
        weight = jnp.concatenate([w_ref[dy, dx] for dy in range(3)], axis=0)
        taps.append(jnp.dot(pieces, weight, preferred_element_type=jnp.float32))
    conv = taps[0] + pltpu.roll(taps[1], total - 1, 0) + pltpu.roll(taps[2], total - 2, 0)
    hidden = (conv / (1.0 + jnp.exp(-conv))).astype(jnp.bfloat16)

    values = hidden.astype(jnp.float32).reshape(frames, count, chans)
    kernel = k_ref[...]
    depth = []
    for t in range(frames):
        acc = values[t] * kernel[0:1]
        for lag in range(1, t + 1):
            acc = acc + values[t - lag] * kernel[lag : lag + 1]
        depth.append(acc.astype(jnp.bfloat16))
    depth = jnp.stack(depth).reshape(total, chans)

    mixed = jnp.dot(depth, p_ref[...], preferred_element_type=jnp.float32).astype(jnp.bfloat16)
    center = pltpu.roll(window(1).astype(jnp.float32), total - 1, 0)
    state = (center + mixed.astype(jnp.float32)).astype(jnp.bfloat16).reshape(frames, count, chans)
    o_ref[...] = jnp.where(m_ref[...][None] > 0, state, jnp.zeros((), state.dtype))


def block(x, weight, kernel, proj, mask, pitch):
    frames, length, chans = x.shape
    count = length - 2 * pitch
    flops = 2 * frames * count * chans * chans * 10
    vmem = pltpu.VMEM
    return pl.pallas_call(
        functools.partial(block_kernel, count=count, pitch=pitch),
        out_shape=jax.ShapeDtypeStruct((frames, count, chans), x.dtype),
        in_specs=[pl.BlockSpec(memory_space=vmem)] * 5,
        out_specs=pl.BlockSpec(memory_space=vmem),
        compiler_params=pltpu.CompilerParams(vmem_limit_bytes=48 * 1024 * 1024),
        cost_estimate=pl.CostEstimate(
            flops=flops,
            transcendentals=frames * count * chans,
            bytes_accessed=2 * frames * (length + count) * chans + 2 * 10 * chans * chans,
        ),
    )(x, weight, kernel, proj, mask)


def shards(video, conv_w, depth_k, proj_w):
    bands = lax.axis_size("tm")
    sides = lax.axis_size("width")
    band = lax.axis_index("tm")
    side = lax.axis_index("width")
    frames, height, cols, chans = video.shape
    rows = height // bands
    halo = BLOCKS
    pitch = -(-(cols + 2 * halo) // LANES) * LANES

    padded = jnp.pad(video, ((0, 0), (halo, halo), (0, 0), (0, 0)))
    pieces = jnp.stack([padded[:, r * rows : r * rows + rows + 2 * halo] for r in range(bands)])
    received = lax.all_to_all(pieces, "tm", 0, 0, tiled=False)

    up = [(i, i + 1) for i in range(sides - 1)]
    down = [(i + 1, i) for i in range(sides - 1)]
    before = lax.ppermute(received[:, :, :, cols - halo :], "width", up)
    after = lax.ppermute(received[:, :, :, :halo], "width", down)
    spare = jnp.zeros(received.shape[:3] + (pitch - cols - 2 * halo, chans), received.dtype)
    state = jnp.concatenate([before, received, after, spare], axis=3)
    state = state.reshape(bands * frames, -1, chans)

    for b in range(BLOCKS):
        left = halo - 1 - b
        n_rows = rows + 2 * left
        row = band * rows - left + lax.broadcasted_iota(jnp.int32, (n_rows, pitch), 0)
        col = side * cols - left + lax.broadcasted_iota(jnp.int32, (n_rows, pitch), 1)
        inside = (row >= 0) & (row < height) & (col >= 0) & (col < sides * cols)
        inside = inside & (lax.broadcasted_iota(jnp.int32, (n_rows, pitch), 1) < cols + 2 * left)
        mask = jnp.broadcast_to(inside.reshape(-1, 1), (n_rows * pitch, chans)).astype(jnp.float32)
        state = block(state, conv_w[b], depth_k[b], proj_w[b], mask, pitch)

    state = state.reshape(state.shape[0], rows, pitch, chans)[:, :, :cols]
    return lax.all_to_all(state, "tm", 0, 1, tiled=True)


def solution(mesh):
    return jax.shard_map(
        shards,
        mesh=mesh,
        in_specs=(P(("groups", "tm"), None, "width", None), P(), P(), P()),
        out_specs=P(("groups", "tm"), None, "width", None),
        check_vma=False,
    )
```

```python
import functools

import jax
import jax.numpy as jnp
from jax import lax
from jax.experimental import pallas as pl
from jax.experimental.pallas import tpu as pltpu
from jax.sharding import PartitionSpec as P

BLOCKS = 2
LANES = 16


def block_kernel(x_ref, w_ref, k_ref, p_ref, m_ref, o_ref, *, count, pitch):
    frames, _, chans = x_ref.shape
    total = frames * count

    def window(dy):
        return x_ref[:, dy * pitch : dy * pitch + count, :].reshape(total, chans)

    taps = [None, None, None]
    for dy in range(3):
        piece = window(dy)
        for dx in range(3):
            part = jnp.dot(piece, w_ref[dy, dx], preferred_element_type=jnp.float32)
            taps[dx] = part if taps[dx] is None else taps[dx] + part
    conv = taps[0] + pltpu.roll(taps[1], total - 1, 0) + pltpu.roll(taps[2], total - 2, 0)
    hidden = (conv / (1.0 + jnp.exp(-conv))).astype(jnp.bfloat16)

    values = hidden.astype(jnp.float32).reshape(frames, count, chans)
    kernel = k_ref[...]
    depth = []
    for t in range(frames):
        acc = values[t] * kernel[0:1]
        for lag in range(1, t + 1):
            acc = acc + values[t - lag] * kernel[lag : lag + 1]
        depth.append(acc.astype(jnp.bfloat16))
    depth = jnp.stack(depth).reshape(total, chans)

    mixed = jnp.dot(depth, p_ref[...], preferred_element_type=jnp.float32).astype(jnp.bfloat16)
    center = pltpu.roll(window(1).astype(jnp.float32), total - 1, 0)
    state = (center + mixed.astype(jnp.float32)).astype(jnp.bfloat16).reshape(frames, count, chans)
    state = jnp.where(m_ref[...][None] > 0, state, jnp.zeros((), state.dtype))
    if o_ref.shape[0] == frames:
        o_ref[...] = state
    else:
        cols = o_ref.shape[1]
        turned = jnp.swapaxes(state.astype(jnp.float32), 0, 1).astype(state.dtype)
        for r in range(o_ref.shape[0]):
            o_ref[r] = turned[r * pitch : r * pitch + cols]


def block(x, weight, kernel, proj, mask, pitch, cols=None):
    frames, length, chans = x.shape
    count = length - 2 * pitch
    shape = (frames, count, chans) if cols is None else (count // pitch, cols, frames, chans)
    flops = 2 * frames * count * chans * chans * 10
    vmem = pltpu.VMEM
    return pl.pallas_call(
        functools.partial(block_kernel, count=count, pitch=pitch),
        out_shape=jax.ShapeDtypeStruct(shape, x.dtype),
        in_specs=[pl.BlockSpec(memory_space=vmem)] * 5,
        out_specs=pl.BlockSpec(memory_space=vmem),
        compiler_params=pltpu.CompilerParams(vmem_limit_bytes=48 * 1024 * 1024),
        cost_estimate=pl.CostEstimate(
            flops=flops,
            transcendentals=frames * count * chans,
            bytes_accessed=2 * frames * (length + count) * chans + 2 * 10 * chans * chans,
        ),
    )(x, weight, kernel, proj, mask)


def shards(video, conv_w, depth_k, proj_w):
    bands = lax.axis_size("tm")
    sides = lax.axis_size("width")
    band = lax.axis_index("tm")
    side = lax.axis_index("width")
    frames, height, cols, chans = video.shape
    rows = height // bands
    halo = BLOCKS
    pitch = -(-(cols + 2 * halo) // LANES) * LANES

    padded = jnp.pad(video, ((0, 0), (halo, halo), (0, 0), (0, 0)))
    pieces = jnp.stack([padded[:, r * rows : r * rows + rows + 2 * halo] for r in range(bands)])
    received = lax.all_to_all(pieces, "tm", 0, 0, tiled=False)

    up = [(i, i + 1) for i in range(sides - 1)]
    down = [(i + 1, i) for i in range(sides - 1)]
    before = lax.ppermute(received[:, :, :, cols - halo :], "width", up)
    after = lax.ppermute(received[:, :, :, :halo], "width", down)
    spare = jnp.zeros(received.shape[:3] + (pitch - cols - 2 * halo, chans), received.dtype)
    state = jnp.concatenate([before, received, after, spare], axis=3)
    state = state.reshape(bands * frames, -1, chans)

    for b in range(BLOCKS):
        left = halo - 1 - b
        n_rows = rows + 2 * left
        row = band * rows - left + lax.broadcasted_iota(jnp.int32, (n_rows, pitch), 0)
        col = side * cols - left + lax.broadcasted_iota(jnp.int32, (n_rows, pitch), 1)
        inside = (row >= 0) & (row < height) & (col >= 0) & (col < sides * cols)
        inside = inside & (lax.broadcasted_iota(jnp.int32, (n_rows, pitch), 1) < cols + 2 * left)
        mask = jnp.broadcast_to(inside.reshape(-1, 1), (n_rows * pitch, chans)).astype(jnp.float32)
        last = b == BLOCKS - 1
        state = block(state, conv_w[b], depth_k[b], proj_w[b], mask, pitch, cols if last else None)

    state = state.reshape(rows, cols, bands, frames, chans)
    state = jnp.transpose(state, (2, 0, 1, 3, 4))
    state = lax.all_to_all(state, "tm", 0, 1, tiled=True)
    return jnp.transpose(state[0], (2, 0, 1, 3))


def solution(mesh):
    return jax.shard_map(
        shards,
        mesh=mesh,
        in_specs=(P(("groups", "tm"), None, "width", None), P(), P(), P()),
        out_specs=P(("groups", "tm"), None, "width", None),
        check_vma=False,
    )
```

```python
import functools

import jax
import numpy as np
import jax.numpy as jnp
from jax import lax
from jax.experimental import pallas as pl
from jax.experimental.pallas import tpu as pltpu
from jax.sharding import PartitionSpec as P

BLOCKS = 2
LANES = 16


def block_kernel(x_ref, w_ref, k_ref, p_ref, m_ref, o_ref, *, count, pitch):
    frames, _, chans = x_ref.shape
    total = frames * count

    def window(dy):
        return x_ref[:, dy * pitch : dy * pitch + count, :].reshape(total, chans)

    taps = [None, None, None]
    for dy in range(3):
        piece = window(dy)
        for dx in range(3):
            part = jnp.dot(piece, w_ref[dy, dx], preferred_element_type=jnp.float32)
            taps[dx] = part if taps[dx] is None else taps[dx] + part
    conv = taps[0] + pltpu.roll(taps[1], total - 1, 0) + pltpu.roll(taps[2], total - 2, 0)
    hidden = (conv / (1.0 + jnp.exp(-conv))).astype(jnp.bfloat16)

    values = hidden.astype(jnp.float32).reshape(frames, count, chans)
    kernel = k_ref[...]
    depth = []
    for t in range(frames):
        acc = values[t] * kernel[0:1]
        for lag in range(1, t + 1):
            acc = acc + values[t - lag] * kernel[lag : lag + 1]
        depth.append(acc.astype(jnp.bfloat16))
    depth = jnp.stack(depth).reshape(total, chans)

    mixed = jnp.dot(depth, p_ref[...], preferred_element_type=jnp.float32).astype(jnp.bfloat16)
    center = pltpu.roll(window(1).astype(jnp.float32), total - 1, 0)
    state = (center + mixed.astype(jnp.float32)).astype(jnp.bfloat16).reshape(frames, count, chans)
    state = jnp.where(m_ref[...][None] > 0, state, jnp.zeros((), state.dtype))
    if o_ref.shape[0] == frames:
        o_ref[...] = state
    else:
        cols = o_ref.shape[1]
        turned = jnp.swapaxes(state.astype(jnp.float32), 0, 1).astype(state.dtype)
        for r in range(o_ref.shape[0]):
            o_ref[r] = turned[r * pitch : r * pitch + cols]


def block(x, weight, kernel, proj, mask, pitch, cols=None):
    frames, length, chans = x.shape
    count = length - 2 * pitch
    shape = (frames, count, chans) if cols is None else (count // pitch, cols, frames, chans)
    flops = 2 * frames * count * chans * chans * 10
    vmem = pltpu.VMEM
    return pl.pallas_call(
        functools.partial(block_kernel, count=count, pitch=pitch),
        out_shape=jax.ShapeDtypeStruct(shape, x.dtype),
        in_specs=[pl.BlockSpec(memory_space=vmem)] * 5,
        out_specs=pl.BlockSpec(memory_space=vmem),
        compiler_params=pltpu.CompilerParams(vmem_limit_bytes=48 * 1024 * 1024),
        cost_estimate=pl.CostEstimate(
            flops=flops,
            transcendentals=frames * count * chans,
            bytes_accessed=2 * frames * (length + count) * chans + 2 * 10 * chans * chans,
        ),
    )(x, weight, kernel, proj, mask)


def shards(video, conv_w, depth_k, proj_w):
    bands = lax.axis_size("tm")
    sides = lax.axis_size("width")
    band = lax.axis_index("tm")
    side = lax.axis_index("width")
    frames, height, cols, chans = video.shape
    rows = height // bands
    halo = BLOCKS
    pitch = -(-(cols + 2 * halo) // LANES) * LANES

    padded = jnp.pad(video, ((0, 0), (halo, halo), (0, 0), (0, 0)))
    picks = np.array([r * rows + i for r in range(bands) for i in range(rows + 2 * halo)], np.int32)
    pieces = jnp.take(padded, picks, axis=1).reshape(frames, bands, rows + 2 * halo, cols, chans)
    pieces = jnp.transpose(pieces, (1, 0, 2, 3, 4))
    received = lax.all_to_all(pieces, "tm", 0, 0, tiled=False)

    up = [(i, i + 1) for i in range(sides - 1)]
    down = [(i + 1, i) for i in range(sides - 1)]
    before = lax.ppermute(received[:, :, :, cols - halo :], "width", up)
    after = lax.ppermute(received[:, :, :, :halo], "width", down)
    spare = jnp.zeros(received.shape[:3] + (pitch - cols - 2 * halo, chans), received.dtype)
    state = jnp.concatenate([before, received, after, spare], axis=3)
    state = state.reshape(bands * frames, -1, chans)

    for b in range(BLOCKS):
        left = halo - 1 - b
        n_rows = rows + 2 * left
        row = band * rows - left + lax.broadcasted_iota(jnp.int32, (n_rows, pitch), 0)
        col = side * cols - left + lax.broadcasted_iota(jnp.int32, (n_rows, pitch), 1)
        inside = (row >= 0) & (row < height) & (col >= 0) & (col < sides * cols)
        inside = inside & (lax.broadcasted_iota(jnp.int32, (n_rows, pitch), 1) < cols + 2 * left)
        mask = jnp.broadcast_to(inside.reshape(-1, 1), (n_rows * pitch, chans)).astype(jnp.float32)
        last = b == BLOCKS - 1
        state = block(state, conv_w[b], depth_k[b], proj_w[b], mask, pitch, cols if last else None)

    state = state.reshape(rows, cols, bands, frames, chans)
    state = jnp.transpose(state, (2, 0, 1, 3, 4))
    state = lax.all_to_all(state, "tm", 0, 1, tiled=True)
    return jnp.transpose(state[0], (2, 0, 1, 3))


def solution(mesh):
    return jax.shard_map(
        shards,
        mesh=mesh,
        in_specs=(P(("groups", "tm"), None, "width", None), P(), P(), P()),
        out_specs=P(("groups", "tm"), None, "width", None),
        check_vma=False,
    )
```

```python
import functools

import jax
import jax.numpy as jnp
from jax import lax
from jax.experimental import pallas as pl
from jax.experimental.pallas import tpu as pltpu
from jax.sharding import PartitionSpec as P

BLOCKS = 2
LANES = 16


def block_kernel(x_ref, w_ref, k_ref, p_ref, m_ref, o_ref, v_ref, d_ref, *, count, pitch):
    frames, _, chans = x_ref.shape
    total = frames * count

    def window(dy):
        return x_ref[:, dy * pitch : dy * pitch + count, :].reshape(total, chans)

    taps = [None, None, None]
    for dy in range(3):
        piece = window(dy)
        for dx in range(3):
            part = jnp.dot(piece, w_ref[dy, dx], preferred_element_type=jnp.float32)
            taps[dx] = part if taps[dx] is None else taps[dx] + part
    conv = taps[0] + pltpu.roll(taps[1], total - 1, 0) + pltpu.roll(taps[2], total - 2, 0)
    hidden = (conv * (0.5 + 0.5 * jnp.tanh(0.5 * conv))).astype(jnp.bfloat16)
    v_ref[...] = hidden.astype(jnp.float32).reshape(frames, count, chans)

    sub, lane = 8, 128
    tiles = (count // sub) * (chans // lane)

    def mix(i, carry):
        rows = pl.ds(pl.multiple_of((i // (chans // lane)) * sub, sub), sub)
        lanes = pl.ds(pl.multiple_of((i % (chans // lane)) * lane, lane), lane)
        values = [v_ref[s, rows, lanes] for s in range(frames)]
        taps_k = [k_ref[lag, :, lanes] for lag in range(frames)]
        for t in range(frames):
            acc = values[t] * taps_k[0]
            for lag in range(1, t + 1):
                acc = acc + values[t - lag] * taps_k[lag]
            d_ref[t, rows, lanes] = acc
        return carry

    lax.fori_loop(0, tiles, mix, 0)
    depth = d_ref[...].astype(jnp.bfloat16).reshape(total, chans)

    mixed = jnp.dot(depth, p_ref[...], preferred_element_type=jnp.float32).astype(jnp.bfloat16)
    center = pltpu.roll(window(1).astype(jnp.float32), total - 1, 0)
    state = (center + mixed.astype(jnp.float32)).astype(jnp.bfloat16).reshape(frames, count, chans)
    state = jnp.where(m_ref[...][None] > 0, state, jnp.zeros((), state.dtype))
    if o_ref.shape[0] == frames:
        o_ref[...] = state
    else:
        cols = o_ref.shape[1]
        turned = jnp.swapaxes(state.astype(jnp.float32), 0, 1).astype(state.dtype)
        for r in range(o_ref.shape[0]):
            o_ref[r] = turned[r * pitch : r * pitch + cols]


def block(x, weight, kernel, proj, mask, pitch, cols=None):
    frames, length, chans = x.shape
    count = length - 2 * pitch
    shape = (frames, count, chans) if cols is None else (count // pitch, cols, frames, chans)
    flops = 2 * frames * count * chans * chans * 10
    vmem = pltpu.VMEM
    return pl.pallas_call(
        functools.partial(block_kernel, count=count, pitch=pitch),
        out_shape=jax.ShapeDtypeStruct(shape, x.dtype),
        in_specs=[pl.BlockSpec(memory_space=vmem)] * 5,
        out_specs=pl.BlockSpec(memory_space=vmem),
        scratch_shapes=[pltpu.VMEM((frames, count, chans), jnp.float32)] * 2,
        compiler_params=pltpu.CompilerParams(vmem_limit_bytes=48 * 1024 * 1024),
        cost_estimate=pl.CostEstimate(
            flops=flops,
            transcendentals=frames * count * chans,
            bytes_accessed=2 * frames * (length + count) * chans + 2 * 10 * chans * chans,
        ),
    )(x, weight, jnp.broadcast_to(kernel[:, None, :], (frames, 8, chans)), proj, mask)


def shards(video, conv_w, depth_k, proj_w):
    bands = lax.axis_size("tm")
    sides = lax.axis_size("width")
    band = lax.axis_index("tm")
    side = lax.axis_index("width")
    frames, height, cols, chans = video.shape
    rows = height // bands
    halo = BLOCKS
    pitch = -(-(cols + 2 * halo) // LANES) * LANES

    padded = jnp.pad(video, ((0, 0), (halo, halo), (0, 0), (0, 0)))
    pieces = jnp.stack([padded[:, r * rows : r * rows + rows + 2 * halo] for r in range(bands)])
    received = lax.all_to_all(pieces, "tm", 0, 0, tiled=False)

    up = [(i, i + 1) for i in range(sides - 1)]
    down = [(i + 1, i) for i in range(sides - 1)]
    before = lax.ppermute(received[:, :, :, cols - halo :], "width", up)
    after = lax.ppermute(received[:, :, :, :halo], "width", down)
    spare = jnp.zeros(received.shape[:3] + (pitch - cols - 2 * halo, chans), received.dtype)
    state = jnp.concatenate([before, received, after, spare], axis=3)
    state = state.reshape(bands * frames, -1, chans)

    for b in range(BLOCKS):
        left = halo - 1 - b
        n_rows = rows + 2 * left
        row = band * rows - left + lax.broadcasted_iota(jnp.int32, (n_rows, pitch), 0)
        col = side * cols - left + lax.broadcasted_iota(jnp.int32, (n_rows, pitch), 1)
        inside = (row >= 0) & (row < height) & (col >= 0) & (col < sides * cols)
        inside = inside & (lax.broadcasted_iota(jnp.int32, (n_rows, pitch), 1) < cols + 2 * left)
        mask = jnp.broadcast_to(inside.reshape(-1, 1), (n_rows * pitch, chans)).astype(jnp.float32)
        last = b == BLOCKS - 1
        state = block(state, conv_w[b], depth_k[b], proj_w[b], mask, pitch, cols if last else None)

    state = state.reshape(rows, cols, bands, frames, chans)
    state = jnp.transpose(state, (2, 0, 1, 3, 4))
    state = lax.all_to_all(state, "tm", 0, 1, tiled=True)
    return jnp.transpose(state[0], (2, 0, 1, 3))


def solution(mesh):
    return jax.shard_map(
        shards,
        mesh=mesh,
        in_specs=(P(("groups", "tm"), None, "width", None), P(), P(), P()),
        out_specs=P(("groups", "tm"), None, "width", None),
        check_vma=False,
    )
```

```python
import functools

import jax
import jax.numpy as jnp
from jax import lax
from jax.experimental import pallas as pl
from jax.experimental.pallas import tpu as pltpu
from jax.sharding import PartitionSpec as P

BLOCKS = 2
LANES = 16


def block_kernel(x_ref, w_ref, k_ref, p_ref, m_ref, o_ref, *, count, pitch):
    frames, _, chans = x_ref.shape
    total = frames * count

    def window(dy):
        return x_ref[:, dy * pitch : dy * pitch + count, :].reshape(total, chans)

    taps = [None, None, None]
    for dy in range(3):
        piece = window(dy)
        for dx in range(3):
            part = jnp.dot(piece, w_ref[dy, dx], preferred_element_type=jnp.float32)
            taps[dx] = part if taps[dx] is None else taps[dx] + part
    conv = taps[0] + pltpu.roll(taps[1], total - 1, 0) + pltpu.roll(taps[2], total - 2, 0)
    hidden = (conv / (1.0 + jnp.exp(-conv))).astype(jnp.bfloat16)

    values = hidden.astype(jnp.float32).reshape(frames, count, chans)
    kernel = k_ref[...]
    depth = []
    for t in range(frames):
        acc = values[t] * kernel[0:1]
        for lag in range(1, t + 1):
            acc = acc + values[t - lag] * kernel[lag : lag + 1]
        depth.append(acc.astype(jnp.bfloat16))
    depth = jnp.stack(depth).reshape(total, chans)

    mixed = jnp.dot(depth, p_ref[...], preferred_element_type=jnp.float32).astype(jnp.bfloat16)
    center = pltpu.roll(window(1).astype(jnp.float32), total - 1, 0)
    state = (center + mixed.astype(jnp.float32)).astype(jnp.bfloat16).reshape(frames, count, chans)
    state = jnp.where(m_ref[...][None] > 0, state, jnp.zeros((), state.dtype))
    if o_ref.shape[0] == frames:
        o_ref[...] = state
    else:
        cols = o_ref.shape[1]
        turned = jnp.swapaxes(state.astype(jnp.float32), 0, 1).astype(state.dtype)
        for r in range(o_ref.shape[0]):
            o_ref[r] = turned[r * pitch : r * pitch + cols]


def block(x, weight, kernel, proj, mask, pitch, cols=None):
    frames, length, chans = x.shape
    count = length - 2 * pitch
    shape = (frames, count, chans) if cols is None else (count // pitch, cols, frames, chans)
    flops = 2 * frames * count * chans * chans * 10
    vmem = pltpu.VMEM
    return pl.pallas_call(
        functools.partial(block_kernel, count=count, pitch=pitch),
        out_shape=jax.ShapeDtypeStruct(shape, x.dtype),
        in_specs=[pl.BlockSpec(memory_space=vmem)] * 5,
        out_specs=pl.BlockSpec(memory_space=vmem),
        compiler_params=pltpu.CompilerParams(vmem_limit_bytes=48 * 1024 * 1024),
        cost_estimate=pl.CostEstimate(
            flops=flops,
            transcendentals=frames * count * chans,
            bytes_accessed=2 * frames * (length + count) * chans + 2 * 10 * chans * chans,
        ),
    )(x, weight, kernel, proj, mask)


def shards(video, conv_w, depth_k, proj_w):
    bands = lax.axis_size("tm")
    sides = lax.axis_size("width")
    band = lax.axis_index("tm")
    side = lax.axis_index("width")
    frames, height, cols, chans = video.shape
    rows = height // bands
    halo = BLOCKS
    pitch = -(-(cols + 2 * halo) // LANES) * LANES

    padded = jnp.pad(video, ((0, 0), (halo, halo), (0, 0), (0, 0)))
    pieces = jnp.stack([padded[:, r * rows : r * rows + rows + 2 * halo] for r in range(bands)])
    received = lax.all_to_all(pieces, "tm", 0, 0, tiled=False)

    up = [(i, i + 1) for i in range(sides - 1)]
    down = [(i + 1, i) for i in range(sides - 1)]
    before = lax.ppermute(received[:, :, :, cols - halo :], "width", up)
    after = lax.ppermute(received[:, :, :, :halo], "width", down)
    state = jnp.pad(received, ((0, 0), (0, 0), (0, 0), (halo, pitch - cols - halo), (0, 0)))
    state = state.reshape(bands * frames, rows + 2 * halo, pitch, chans)
    edge = (bands * frames, rows + 2 * halo, halo, chans)
    state = lax.dynamic_update_slice(state, before.reshape(edge), (0, 0, 0, 0))
    state = lax.dynamic_update_slice(state, after.reshape(edge), (0, 0, halo + cols, 0))
    state = state.reshape(bands * frames, -1, chans)

    for b in range(BLOCKS):
        left = halo - 1 - b
        n_rows = rows + 2 * left
        row = band * rows - left + lax.broadcasted_iota(jnp.int32, (n_rows, pitch), 0)
        col = side * cols - left + lax.broadcasted_iota(jnp.int32, (n_rows, pitch), 1)
        inside = (row >= 0) & (row < height) & (col >= 0) & (col < sides * cols)
        inside = inside & (lax.broadcasted_iota(jnp.int32, (n_rows, pitch), 1) < cols + 2 * left)
        mask = jnp.broadcast_to(inside.reshape(-1, 1), (n_rows * pitch, chans)).astype(jnp.float32)
        last = b == BLOCKS - 1
        state = block(state, conv_w[b], depth_k[b], proj_w[b], mask, pitch, cols if last else None)

    state = state.reshape(rows, cols, bands, frames, chans)
    state = jnp.transpose(state, (2, 0, 1, 3, 4))
    state = lax.all_to_all(state, "tm", 0, 1, tiled=True)
    return jnp.transpose(state[0], (2, 0, 1, 3))


def solution(mesh):
    return jax.shard_map(
        shards,
        mesh=mesh,
        in_specs=(P(("groups", "tm"), None, "width", None), P(), P(), P()),
        out_specs=P(("groups", "tm"), None, "width", None),
        check_vma=False,
    )
```

```python
import functools

import jax
import jax.numpy as jnp
from jax import lax
from jax.experimental import pallas as pl
from jax.experimental.pallas import tpu as pltpu
from jax.sharding import PartitionSpec as P

BLOCKS = 2
LANES = 16


def block_kernel(x_ref, w_ref, k_ref, p_ref, m_ref, o_ref, *, count, pitch):
    frames, _, chans = x_ref.shape
    total = frames * count

    def window(dy):
        return x_ref[:, dy * pitch : dy * pitch + count, :].reshape(total, chans)

    def operand(dy):
        return window(dy).astype(jnp.bfloat16)

    taps = [None, None, None]
    for dy in range(3):
        piece = operand(dy)
        for dx in range(3):
            part = jnp.dot(piece, w_ref[dy, dx], preferred_element_type=jnp.float32)
            taps[dx] = part if taps[dx] is None else taps[dx] + part
    conv = taps[0] + pltpu.roll(taps[1], total - 1, 0) + pltpu.roll(taps[2], total - 2, 0)
    hidden = (conv / (1.0 + jnp.exp(-conv))).astype(jnp.bfloat16)

    values = hidden.astype(jnp.float32).reshape(frames, count, chans)
    kernel = k_ref[...]
    depth = []
    for t in range(frames):
        acc = values[t] * kernel[0:1]
        for lag in range(1, t + 1):
            acc = acc + values[t - lag] * kernel[lag : lag + 1]
        depth.append(acc.astype(jnp.bfloat16) if count % 16 == 0 else acc)
    depth = jnp.stack(depth).reshape(total, chans).astype(jnp.bfloat16)

    mixed = jnp.dot(depth, p_ref[...], preferred_element_type=jnp.float32).astype(jnp.bfloat16)
    center = pltpu.roll(window(1).astype(jnp.float32), total - 1, 0)
    state = (center + mixed.astype(jnp.float32)).astype(jnp.bfloat16).astype(o_ref.dtype)
    state = state.reshape(frames, count, chans)
    state = jnp.where(m_ref[...][None] > 0, state, jnp.zeros((), state.dtype))
    if o_ref.shape[0] == frames:
        o_ref[...] = state
    else:
        cols = o_ref.shape[1]
        turned = jnp.swapaxes(state.astype(jnp.float32), 0, 1).astype(state.dtype)
        for r in range(o_ref.shape[0]):
            o_ref[r] = turned[r * pitch : r * pitch + cols]


def block(x, weight, kernel, proj, mask, pitch, cols=None):
    frames, length, chans = x.shape
    count = length - 2 * pitch
    shape = (frames, count, chans) if cols is None else (count // pitch, cols, frames, chans)
    dtype = x.dtype if cols is None else jnp.bfloat16
    flops = 2 * frames * count * chans * chans * 10
    vmem = pltpu.VMEM
    return pl.pallas_call(
        functools.partial(block_kernel, count=count, pitch=pitch),
        out_shape=jax.ShapeDtypeStruct(shape, dtype),
        in_specs=[pl.BlockSpec(memory_space=vmem)] * 5,
        out_specs=pl.BlockSpec(memory_space=vmem),
        compiler_params=pltpu.CompilerParams(vmem_limit_bytes=48 * 1024 * 1024),
        cost_estimate=pl.CostEstimate(
            flops=flops,
            transcendentals=frames * count * chans,
            bytes_accessed=x.dtype.itemsize * frames * (length + count) * chans + 2 * 10 * chans * chans,
        ),
    )(x, weight, kernel, proj, mask)


def shards(video, conv_w, depth_k, proj_w):
    bands = lax.axis_size("tm")
    sides = lax.axis_size("width")
    band = lax.axis_index("tm")
    side = lax.axis_index("width")
    frames, height, cols, chans = video.shape
    rows = height // bands
    halo = BLOCKS
    pitch = -(-(cols + 2 * halo) // LANES) * LANES

    padded = jnp.pad(video, ((0, 0), (halo, halo), (0, 0), (0, 0)))
    pieces = jnp.stack([padded[:, r * rows : r * rows + rows + 2 * halo] for r in range(bands)])
    received = lax.all_to_all(pieces, "tm", 0, 0, tiled=False)

    up = [(i, i + 1) for i in range(sides - 1)]
    down = [(i + 1, i) for i in range(sides - 1)]
    before = lax.ppermute(received[:, :, :, cols - halo :], "width", up)
    after = lax.ppermute(received[:, :, :, :halo], "width", down)
    def image_mask(left, width, first):
        n_rows = rows + 2 * left
        row = band * rows - left + lax.broadcasted_iota(jnp.int32, (n_rows, width), 0)
        col = side * cols + first + lax.broadcasted_iota(jnp.int32, (n_rows, width), 1)
        inside = (row >= 0) & (row < height) & (col >= 0) & (col < sides * cols)
        return jnp.broadcast_to(inside.reshape(-1, 1), (n_rows * width, chans)).astype(jnp.float32)

    band_in = jnp.pad(received, ((0, 0), (0, 0), (0, 0), (halo, pitch - cols - halo), (0, 0)))
    band_in = band_in.reshape(bands * frames, -1, chans)
    cut = (jnp.arange(pitch) < cols + 2 * (halo - 1)).astype(jnp.float32)
    first_mask = image_mask(halo - 1, pitch, -(halo - 1)) * jnp.tile(cut, rows + 2 * (halo - 1))[:, None]
    state = block(band_in, conv_w[0], depth_k[0], proj_w[0], first_mask, pitch)

    reach = 2 * halo
    rim = jnp.concatenate([before, received[:, :, :, :halo], received[:, :, :, cols - halo :], after], axis=3)
    rim = rim.astype(jnp.float32).reshape(bands * frames, -1, chans)
    rim_left = image_mask(halo - 1, halo, -(halo - 1))
    rim_right = image_mask(halo - 1, halo, cols - 1)
    n_rows = rows + 2 * (halo - 1)
    rim_mask = jnp.concatenate(
        [rim_left.reshape(n_rows, halo, chans), jnp.zeros((n_rows, halo, chans), jnp.float32),
         rim_right.reshape(n_rows, halo, chans), jnp.zeros((n_rows, halo, chans), jnp.float32)], axis=1
    ).reshape(-1, chans)
    rims = block(rim, conv_w[0], depth_k[0], proj_w[0], rim_mask, 2 * reach)
    rims = rims.astype(state.dtype).reshape(bands * frames, n_rows, 2 * reach, chans)
    state = state.reshape(bands * frames, n_rows, pitch, chans)
    state = lax.dynamic_update_slice(state, rims[:, :, :halo], (0, 0, 0, 0))
    state = lax.dynamic_update_slice(state, rims[:, :, reach : reach + halo], (0, 0, cols + halo - 2 * (halo - 1), 0))
    state = state.reshape(bands * frames, -1, chans)

    for b in range(1, BLOCKS):
        left = halo - 1 - b
        mask = image_mask(left, pitch, -left)
        last = b == BLOCKS - 1
        state = block(state, conv_w[b], depth_k[b], proj_w[b], mask, pitch, cols if last else None)

    state = state.reshape(rows, cols, bands, frames, chans)
    state = jnp.transpose(state, (2, 0, 1, 3, 4))
    state = lax.all_to_all(state, "tm", 0, 1, tiled=True)
    return jnp.transpose(state[0], (2, 0, 1, 3))


def solution(mesh):
    return jax.shard_map(
        shards,
        mesh=mesh,
        in_specs=(P(("groups", "tm"), None, "width", None), P(), P(), P()),
        out_specs=P(("groups", "tm"), None, "width", None),
        check_vma=False,
    )
```

```python
import functools

import jax
import jax.numpy as jnp
from jax import lax
from jax.experimental import pallas as pl
from jax.experimental.pallas import tpu as pltpu
from jax.sharding import PartitionSpec as P

BLOCKS = 2
LANES = 16


def block_kernel(x_ref, w_ref, k_ref, p_ref, m_ref, o_ref, *, count, pitch):
    frames, _, chans = x_ref.shape
    total = frames * count

    def window(dy):
        return x_ref[:, dy * pitch : dy * pitch + count, :].reshape(total, chans)

    def operand(dy):
        return window(dy).astype(jnp.bfloat16)

    taps = [None, None, None]
    for dy in range(3):
        piece = operand(dy)
        for dx in range(3):
            part = jnp.dot(piece, w_ref[dy, dx], preferred_element_type=jnp.float32)
            taps[dx] = part if taps[dx] is None else taps[dx] + part
    conv = taps[0] + pltpu.roll(taps[1], total - 1, 0) + pltpu.roll(taps[2], total - 2, 0)
    hidden = (conv * (0.5 + 0.5 * jnp.tanh(0.5 * conv))).astype(jnp.bfloat16)

    values = hidden.astype(jnp.float32).reshape(frames, count, chans)
    kernel = k_ref[...]
    depth = []
    for t in range(frames):
        acc = values[t] * kernel[0:1]
        for lag in range(1, t + 1):
            acc = acc + values[t - lag] * kernel[lag : lag + 1]
        depth.append(acc.astype(jnp.bfloat16) if count % 16 == 0 else acc)
    depth = jnp.stack(depth).reshape(total, chans).astype(jnp.bfloat16)

    mixed = jnp.dot(depth, p_ref[...], preferred_element_type=jnp.float32).astype(jnp.bfloat16)
    center = pltpu.roll(window(1).astype(jnp.float32), total - 1, 0)
    state = (center + mixed.astype(jnp.float32)).astype(jnp.bfloat16).astype(o_ref.dtype)
    state = state.reshape(frames, count, chans)
    state = jnp.where(m_ref[...][None] > 0, state, jnp.zeros((), state.dtype))
    if o_ref.shape[0] == frames:
        o_ref[...] = state
    else:
        cols = o_ref.shape[1]
        turned = jnp.swapaxes(state.astype(jnp.float32), 0, 1).astype(state.dtype)
        for r in range(o_ref.shape[0]):
            o_ref[r] = turned[r * pitch : r * pitch + cols]


def block(x, weight, kernel, proj, mask, pitch, cols=None):
    frames, length, chans = x.shape
    count = length - 2 * pitch
    shape = (frames, count, chans) if cols is None else (count // pitch, cols, frames, chans)
    dtype = x.dtype if cols is None else jnp.bfloat16
    flops = 2 * frames * count * chans * chans * 10
    vmem = pltpu.VMEM
    return pl.pallas_call(
        functools.partial(block_kernel, count=count, pitch=pitch),
        out_shape=jax.ShapeDtypeStruct(shape, dtype),
        in_specs=[pl.BlockSpec(memory_space=vmem)] * 5,
        out_specs=pl.BlockSpec(memory_space=vmem),
        compiler_params=pltpu.CompilerParams(vmem_limit_bytes=48 * 1024 * 1024),
        cost_estimate=pl.CostEstimate(
            flops=flops,
            transcendentals=frames * count * chans,
            bytes_accessed=x.dtype.itemsize * frames * (length + count) * chans + 2 * 10 * chans * chans,
        ),
    )(x, weight, kernel, proj, mask)


def shards(video, conv_w, depth_k, proj_w):
    bands = lax.axis_size("tm")
    sides = lax.axis_size("width")
    band = lax.axis_index("tm")
    side = lax.axis_index("width")
    frames, height, cols, chans = video.shape
    rows = height // bands
    halo = BLOCKS
    pitch = -(-(cols + 2 * halo) // LANES) * LANES

    padded = jnp.pad(video, ((0, 0), (halo, halo), (0, 0), (0, 0)))
    pieces = jnp.stack([padded[:, r * rows : r * rows + rows + 2 * halo] for r in range(bands)])
    received = lax.all_to_all(pieces, "tm", 0, 0, tiled=False)

    up = [(i, i + 1) for i in range(sides - 1)]
    down = [(i + 1, i) for i in range(sides - 1)]
    before = lax.ppermute(received[:, :, :, cols - halo :], "width", up)
    after = lax.ppermute(received[:, :, :, :halo], "width", down)
    def image_mask(left, width, first):
        n_rows = rows + 2 * left
        row = band * rows - left + lax.broadcasted_iota(jnp.int32, (n_rows, width), 0)
        col = side * cols + first + lax.broadcasted_iota(jnp.int32, (n_rows, width), 1)
        inside = (row >= 0) & (row < height) & (col >= 0) & (col < sides * cols)
        return jnp.broadcast_to(inside.reshape(-1, 1), (n_rows * width, chans)).astype(jnp.float32)

    band_in = jnp.pad(received, ((0, 0), (0, 0), (0, 0), (halo, pitch - cols - halo), (0, 0)))
    band_in = band_in.reshape(bands * frames, -1, chans)
    cut = (jnp.arange(pitch) < cols + 2 * (halo - 1)).astype(jnp.float32)
    first_mask = image_mask(halo - 1, pitch, -(halo - 1)) * jnp.tile(cut, rows + 2 * (halo - 1))[:, None]
    state = block(band_in, conv_w[0], depth_k[0], proj_w[0], first_mask, pitch)

    reach = 2 * halo
    rim = jnp.concatenate([received[:, :, :, :halo], received[:, :, :, cols - halo :]], axis=3).astype(jnp.float32)
    rim = jnp.pad(rim, ((0, 0), (0, 0), (0, 0), (halo, halo), (0, 0)))
    rim = rim.reshape((bands * frames,) + rim.shape[2:])
    edge = (bands * frames, rows + 2 * halo, halo, chans)
    rim = lax.dynamic_update_slice(rim, before.astype(jnp.float32).reshape(edge), (0, 0, 0, 0))
    rim = lax.dynamic_update_slice(rim, after.astype(jnp.float32).reshape(edge), (0, 0, 3 * halo, 0))
    rim = rim.reshape(bands * frames, -1, chans)
    rim_left = image_mask(halo - 1, halo, -(halo - 1))
    rim_right = image_mask(halo - 1, halo, cols - 1)
    n_rows = rows + 2 * (halo - 1)
    rim_mask = jnp.concatenate(
        [rim_left.reshape(n_rows, halo, chans), jnp.zeros((n_rows, halo, chans), jnp.float32),
         rim_right.reshape(n_rows, halo, chans), jnp.zeros((n_rows, halo, chans), jnp.float32)], axis=1
    ).reshape(-1, chans)
    rims = block(rim, conv_w[0], depth_k[0], proj_w[0], rim_mask, 2 * reach)
    rims = rims.astype(state.dtype).reshape(bands * frames, n_rows, 2 * reach, chans)
    state = state.reshape(bands * frames, n_rows, pitch, chans)
    state = lax.dynamic_update_slice(state, rims[:, :, :halo], (0, 0, 0, 0))
    state = lax.dynamic_update_slice(state, rims[:, :, reach : reach + halo], (0, 0, cols + halo - 2 * (halo - 1), 0))
    state = state.reshape(bands * frames, -1, chans)

    for b in range(1, BLOCKS):
        left = halo - 1 - b
        mask = image_mask(left, pitch, -left)
        last = b == BLOCKS - 1
        state = block(state, conv_w[b], depth_k[b], proj_w[b], mask, pitch, cols if last else None)

    state = state.reshape(rows, cols, bands, frames, chans)
    state = jnp.transpose(state, (2, 0, 1, 3, 4))
    state = lax.all_to_all(state, "tm", 0, 1, tiled=True)
    return jnp.transpose(state[0], (2, 0, 1, 3))


def solution(mesh):
    return jax.shard_map(
        shards,
        mesh=mesh,
        in_specs=(P(("groups", "tm"), None, "width", None), P(), P(), P()),
        out_specs=P(("groups", "tm"), None, "width", None),
        check_vma=False,
    )
```

```python
import functools

import jax
import jax.numpy as jnp
from jax import lax
from jax.experimental import pallas as pl
from jax.experimental.pallas import tpu as pltpu
from jax.sharding import PartitionSpec as P

BLOCKS = 2
LANES = 16


def block_kernel(x_ref, w_ref, k_ref, p_ref, m_ref, o_ref, *, count, pitch):
    frames, _, chans = x_ref.shape
    total = frames * count

    def window(dy):
        return x_ref[:, dy * pitch : dy * pitch + count, :].reshape(total, chans)

    def operand(dy):
        return window(dy).astype(jnp.bfloat16)

    taps = [None, None, None]
    for dy in range(3):
        piece = operand(dy)
        for dx in range(3):
            part = jnp.dot(piece, w_ref[dy, dx], preferred_element_type=jnp.float32)
            taps[dx] = part if taps[dx] is None else taps[dx] + part
    conv = taps[0] + pltpu.roll(taps[1], total - 1, 0) + pltpu.roll(taps[2], total - 2, 0)
    hidden = (conv * (0.5 + 0.5 * jnp.tanh(0.5 * conv))).astype(jnp.bfloat16)

    values = hidden.astype(jnp.float32).reshape(frames, count, chans)
    kernel = k_ref[...]
    depth = []
    for t in range(frames):
        acc = values[t] * kernel[0:1]
        for lag in range(1, t + 1):
            acc = acc + values[t - lag] * kernel[lag : lag + 1]
        depth.append(acc.astype(jnp.bfloat16) if count % 16 == 0 else acc)
    depth = jnp.stack(depth).reshape(total, chans).astype(jnp.bfloat16)

    mixed = jnp.dot(depth, p_ref[...], preferred_element_type=jnp.float32).astype(jnp.bfloat16)
    center = pltpu.roll(window(1).astype(jnp.float32), total - 1, 0)
    state = (center + mixed.astype(jnp.float32)).astype(jnp.bfloat16).astype(o_ref.dtype)
    state = state.reshape(frames, count, chans)
    state = jnp.where(m_ref[...][None] > 0, state, jnp.zeros((), state.dtype))
    if o_ref.shape[0] == frames:
        o_ref[...] = state
    else:
        cols = o_ref.shape[1]
        turned = jnp.swapaxes(state.astype(jnp.float32), 0, 1).astype(state.dtype)
        for r in range(o_ref.shape[0]):
            o_ref[r] = turned[r * pitch : r * pitch + cols]


def block(x, weight, kernel, proj, mask, pitch, cols=None):
    frames, length, chans = x.shape
    count = length - 2 * pitch
    shape = (frames, count, chans) if cols is None else (count // pitch, cols, frames, chans)
    dtype = x.dtype if cols is None else jnp.bfloat16
    flops = 2 * frames * count * chans * chans * 10
    vmem = pltpu.VMEM
    return pl.pallas_call(
        functools.partial(block_kernel, count=count, pitch=pitch),
        out_shape=jax.ShapeDtypeStruct(shape, dtype),
        in_specs=[pl.BlockSpec(memory_space=vmem)] * 5,
        out_specs=pl.BlockSpec(memory_space=vmem),
        compiler_params=pltpu.CompilerParams(vmem_limit_bytes=48 * 1024 * 1024),
        cost_estimate=pl.CostEstimate(
            flops=flops,
            transcendentals=frames * count * chans,
            bytes_accessed=x.dtype.itemsize * frames * (length + count) * chans + 2 * 10 * chans * chans,
        ),
    )(x, weight, kernel, proj, mask)


def shards(video, conv_w, depth_k, proj_w):
    bands = lax.axis_size("tm")
    sides = lax.axis_size("width")
    band = lax.axis_index("tm")
    side = lax.axis_index("width")
    frames, height, cols, chans = video.shape
    rows = height // bands
    halo = BLOCKS
    pitch = -(-(cols + 2 * halo) // LANES) * LANES

    padded = jnp.pad(video, ((0, 0), (halo, halo), (0, 0), (0, 0)))
    pieces = jnp.stack([padded[:, r * rows : r * rows + rows + 2 * halo] for r in range(bands)])
    received = lax.all_to_all(pieces, "tm", 0, 0, tiled=False)

    up = [(i, i + 1) for i in range(sides - 1)]
    down = [(i + 1, i) for i in range(sides - 1)]
    before = lax.ppermute(received[:, :, :, cols - halo :], "width", up)
    after = lax.ppermute(received[:, :, :, :halo], "width", down)
    def image_mask(left, width, first):
        n_rows = rows + 2 * left
        row = band * rows - left + lax.broadcasted_iota(jnp.int32, (n_rows, width), 0)
        col = side * cols + first + lax.broadcasted_iota(jnp.int32, (n_rows, width), 1)
        inside = (row >= 0) & (row < height) & (col >= 0) & (col < sides * cols)
        return jnp.broadcast_to(inside.reshape(-1, 1), (n_rows * width, chans)).astype(jnp.float32)

    band_in = jnp.pad(received, ((0, 0), (0, 0), (0, 0), (halo, pitch - cols - halo), (0, 0)))
    band_in = band_in.reshape(bands * frames, -1, chans)
    cut = (jnp.arange(pitch) < cols + 2 * (halo - 1)).astype(jnp.float32)
    first_mask = image_mask(halo - 1, pitch, -(halo - 1)) * jnp.tile(cut, rows + 2 * (halo - 1))[:, None]
    state = block(band_in, conv_w[0], depth_k[0], proj_w[0], first_mask, pitch)

    reach = 2 * halo
    late, before = lax.optimization_barrier((received, before))
    rim = jnp.concatenate([late[:, :, :, :halo], late[:, :, :, cols - halo :]], axis=3).astype(jnp.float32)
    rim = jnp.pad(rim, ((0, 0), (0, 0), (0, 0), (halo, halo), (0, 0)))
    rim = rim.reshape((bands * frames,) + rim.shape[2:])
    edge = (bands * frames, rows + 2 * halo, halo, chans)
    rim = lax.dynamic_update_slice(rim, before.astype(jnp.float32).reshape(edge), (0, 0, 0, 0))
    rim = lax.dynamic_update_slice(rim, after.astype(jnp.float32).reshape(edge), (0, 0, 3 * halo, 0))
    rim = rim.reshape(bands * frames, -1, chans)
    rim_left = image_mask(halo - 1, halo, -(halo - 1))
    rim_right = image_mask(halo - 1, halo, cols - 1)
    n_rows = rows + 2 * (halo - 1)
    rim_mask = jnp.concatenate(
        [rim_left.reshape(n_rows, halo, chans), jnp.zeros((n_rows, halo, chans), jnp.float32),
         rim_right.reshape(n_rows, halo, chans), jnp.zeros((n_rows, halo, chans), jnp.float32)], axis=1
    ).reshape(-1, chans)
    rims = block(rim, conv_w[0], depth_k[0], proj_w[0], rim_mask, 2 * reach)
    rims = rims.astype(state.dtype).reshape(bands * frames, n_rows, 2 * reach, chans)
    state = state.reshape(bands * frames, n_rows, pitch, chans)
    state = lax.dynamic_update_slice(state, rims[:, :, :halo], (0, 0, 0, 0))
    state = lax.dynamic_update_slice(state, rims[:, :, reach : reach + halo], (0, 0, cols + halo - 2 * (halo - 1), 0))
    state = state.reshape(bands * frames, -1, chans)

    for b in range(1, BLOCKS):
        left = halo - 1 - b
        mask = image_mask(left, pitch, -left)
        last = b == BLOCKS - 1
        state = block(state, conv_w[b], depth_k[b], proj_w[b], mask, pitch, cols if last else None)

    state = state.reshape(rows, cols, bands, frames, chans)
    state = jnp.transpose(state, (2, 0, 1, 3, 4))
    state = lax.all_to_all(state, "tm", 0, 1, tiled=True)
    return jnp.transpose(state[0], (2, 0, 1, 3))


def solution(mesh):
    return jax.shard_map(
        shards,
        mesh=mesh,
        in_specs=(P(("groups", "tm"), None, "width", None), P(), P(), P()),
        out_specs=P(("groups", "tm"), None, "width", None),
        check_vma=False,
    )
```

```python
import functools

import jax
import jax.numpy as jnp
from jax import lax
from jax.experimental import pallas as pl
from jax.experimental.pallas import tpu as pltpu
from jax.sharding import PartitionSpec as P

BLOCKS = 2
LANES = 16


def block_kernel(x_ref, w_ref, k_ref, p_ref, m_ref, o_ref, *, count, pitch):
    frames, _, chans = x_ref.shape
    total = frames * count

    def window(dy):
        return x_ref[:, dy * pitch : dy * pitch + count, :].reshape(total, chans)

    def operand(dy):
        return window(dy).astype(jnp.bfloat16)

    taps = [None, None, None]
    for dy in range(3):
        piece = operand(dy)
        for dx in range(3):
            part = jnp.dot(piece, w_ref[dy, dx], preferred_element_type=jnp.float32)
            taps[dx] = part if taps[dx] is None else taps[dx] + part
    conv = taps[0] + pltpu.roll(taps[1], total - 1, 0) + pltpu.roll(taps[2], total - 2, 0)
    hidden = (conv * (0.5 + 0.5 * jnp.tanh(0.5 * conv))).astype(jnp.bfloat16)

    values = hidden.astype(jnp.float32).reshape(frames, count, chans)
    kernel = k_ref[...]
    depth = []
    for t in range(frames):
        acc = values[t] * kernel[0:1]
        for lag in range(1, t + 1):
            acc = acc + values[t - lag] * kernel[lag : lag + 1]
        depth.append(acc.astype(jnp.bfloat16) if count % 16 == 0 else acc)
    depth = jnp.stack(depth).reshape(total, chans).astype(jnp.bfloat16)

    mixed = jnp.dot(depth, p_ref[...], preferred_element_type=jnp.float32).astype(jnp.bfloat16)
    center = pltpu.roll(window(1).astype(jnp.float32), total - 1, 0)
    state = (center + mixed.astype(jnp.float32)).astype(jnp.bfloat16).astype(o_ref.dtype)
    state = state.reshape(frames, count, chans)
    state = jnp.where(m_ref[...][None] > 0, state, jnp.zeros((), state.dtype))
    if o_ref.shape[0] == frames:
        o_ref[...] = state
    else:
        cols = o_ref.shape[1]
        turned = jnp.swapaxes(state.astype(jnp.float32), 0, 1).astype(state.dtype)
        for r in range(o_ref.shape[0]):
            o_ref[r] = turned[r * pitch : r * pitch + cols]


def block(x, weight, kernel, proj, mask, pitch, cols=None):
    frames, length, chans = x.shape
    count = length - 2 * pitch
    shape = (frames, count, chans) if cols is None else (count // pitch, cols, frames, chans)
    dtype = x.dtype if cols is None else jnp.bfloat16
    flops = 2 * frames * count * chans * chans * 10
    vmem = pltpu.VMEM
    return pl.pallas_call(
        functools.partial(block_kernel, count=count, pitch=pitch),
        out_shape=jax.ShapeDtypeStruct(shape, dtype),
        in_specs=[pl.BlockSpec(memory_space=vmem)] * 5,
        out_specs=pl.BlockSpec(memory_space=vmem),
        compiler_params=pltpu.CompilerParams(vmem_limit_bytes=48 * 1024 * 1024),
        cost_estimate=pl.CostEstimate(
            flops=flops,
            transcendentals=frames * count * chans,
            bytes_accessed=x.dtype.itemsize * frames * (length + count) * chans + 2 * 10 * chans * chans,
        ),
    )(x, weight, kernel, proj, mask)


def shards(video, conv_w, depth_k, proj_w):
    bands = lax.axis_size("tm")
    sides = lax.axis_size("width")
    band = lax.axis_index("tm")
    side = lax.axis_index("width")
    frames, height, cols, chans = video.shape
    rows = height // bands
    halo = BLOCKS
    pitch = -(-(cols + 2 * halo) // LANES) * LANES

    padded = jnp.pad(video, ((0, 0), (halo, halo), (0, 0), (0, 0)))
    pieces = jnp.stack([padded[:, r * rows : r * rows + rows + 2 * halo] for r in range(bands)])
    received = lax.all_to_all(pieces, "tm", 0, 0, tiled=False)

    up = [(i, i + 1) for i in range(sides - 1)]
    down = [(i + 1, i) for i in range(sides - 1)]
    after = lax.ppermute(received[:, :, :, :halo], "width", down)
    before = lax.ppermute(received[:, :, :, cols - halo :], "width", up)
    def image_mask(left, width, first):
        n_rows = rows + 2 * left
        row = band * rows - left + lax.broadcasted_iota(jnp.int32, (n_rows, width), 0)
        col = side * cols + first + lax.broadcasted_iota(jnp.int32, (n_rows, width), 1)
        inside = (row >= 0) & (row < height) & (col >= 0) & (col < sides * cols)
        return jnp.broadcast_to(inside.reshape(-1, 1), (n_rows * width, chans)).astype(jnp.float32)

    band_in = jnp.pad(received, ((0, 0), (0, 0), (0, 0), (halo, pitch - cols - halo), (0, 0)))
    band_in = band_in.reshape(bands * frames, -1, chans)
    cut = (jnp.arange(pitch) < cols + 2 * (halo - 1)).astype(jnp.float32)
    first_mask = image_mask(halo - 1, pitch, -(halo - 1)) * jnp.tile(cut, rows + 2 * (halo - 1))[:, None]
    state = block(band_in, conv_w[0], depth_k[0], proj_w[0], first_mask, pitch)

    reach = 2 * halo
    late, after = lax.optimization_barrier((received, after))
    rim = jnp.concatenate([late[:, :, :, :halo], late[:, :, :, cols - halo :]], axis=3).astype(jnp.float32)
    rim = jnp.pad(rim, ((0, 0), (0, 0), (0, 0), (halo, halo), (0, 0)))
    rim = rim.reshape((bands * frames,) + rim.shape[2:])
    edge = (bands * frames, rows + 2 * halo, halo, chans)
    rim = lax.dynamic_update_slice(rim, before.astype(jnp.float32).reshape(edge), (0, 0, 0, 0))
    rim = lax.dynamic_update_slice(rim, after.astype(jnp.float32).reshape(edge), (0, 0, 3 * halo, 0))
    rim = rim.reshape(bands * frames, -1, chans)
    rim_left = image_mask(halo - 1, halo, -(halo - 1))
    rim_right = image_mask(halo - 1, halo, cols - 1)
    n_rows = rows + 2 * (halo - 1)
    rim_mask = jnp.concatenate(
        [rim_left.reshape(n_rows, halo, chans), jnp.zeros((n_rows, halo, chans), jnp.float32),
         rim_right.reshape(n_rows, halo, chans), jnp.zeros((n_rows, halo, chans), jnp.float32)], axis=1
    ).reshape(-1, chans)
    rims = block(rim, conv_w[0], depth_k[0], proj_w[0], rim_mask, 2 * reach)
    rims = rims.astype(state.dtype).reshape(bands * frames, n_rows, 2 * reach, chans)
    state = state.reshape(bands * frames, n_rows, pitch, chans)
    state = lax.dynamic_update_slice(state, rims[:, :, :halo], (0, 0, 0, 0))
    state = lax.dynamic_update_slice(state, rims[:, :, reach : reach + halo], (0, 0, cols + halo - 2 * (halo - 1), 0))
    state = state.reshape(bands * frames, -1, chans)

    for b in range(1, BLOCKS):
        left = halo - 1 - b
        mask = image_mask(left, pitch, -left)
        last = b == BLOCKS - 1
        state = block(state, conv_w[b], depth_k[b], proj_w[b], mask, pitch, cols if last else None)

    state = state.reshape(rows, cols, bands, frames, chans)
    state = jnp.transpose(state, (2, 0, 1, 3, 4))
    state = lax.all_to_all(state, "tm", 0, 1, tiled=True)
    return jnp.transpose(state[0], (2, 0, 1, 3))


def solution(mesh):
    return jax.shard_map(
        shards,
        mesh=mesh,
        in_specs=(P(("groups", "tm"), None, "width", None), P(), P(), P()),
        out_specs=P(("groups", "tm"), None, "width", None),
        check_vma=False,
    )
```

```python
import functools

import jax
import jax.numpy as jnp
from jax import lax
from jax.experimental import pallas as pl
from jax.experimental.pallas import tpu as pltpu
from jax.sharding import PartitionSpec as P

BLOCKS = 2
LANES = 16


def block_kernel(x_ref, w_ref, k_ref, p_ref, m_ref, o_ref, *, count, pitch):
    frames, _, chans = x_ref.shape
    total = frames * count

    def window(dy):
        return x_ref[:, dy * pitch : dy * pitch + count, :].reshape(total, chans)

    def operand(dy):
        return window(dy).astype(jnp.bfloat16)

    taps = [None, None, None]
    for dy in range(3):
        piece = operand(dy)
        for dx in range(3):
            part = jnp.dot(piece, w_ref[dy, dx], preferred_element_type=jnp.float32)
            taps[dx] = part if taps[dx] is None else taps[dx] + part
    conv = taps[0] + pltpu.roll(taps[1], total - 1, 0) + pltpu.roll(taps[2], total - 2, 0)
    hidden = (conv * (0.5 + 0.5 * jnp.tanh(0.5 * conv))).astype(jnp.bfloat16)

    values = hidden.astype(jnp.float32).reshape(frames, count, chans)
    kernel = k_ref[...]
    depth = []
    for t in range(frames):
        acc = values[t] * kernel[0:1]
        for lag in range(1, t + 1):
            acc = acc + values[t - lag] * kernel[lag : lag + 1]
        depth.append(acc.astype(jnp.bfloat16) if count % 16 == 0 else acc)
    depth = jnp.stack(depth).reshape(total, chans).astype(jnp.bfloat16)

    mixed = jnp.dot(depth, p_ref[...], preferred_element_type=jnp.float32).astype(jnp.bfloat16)
    center = pltpu.roll(window(1).astype(jnp.float32), total - 1, 0)
    state = (center + mixed.astype(jnp.float32)).astype(jnp.bfloat16).astype(o_ref.dtype)
    state = state.reshape(frames, count, chans)
    state = jnp.where(m_ref[...][None] > 0, state, jnp.zeros((), state.dtype))
    if o_ref.shape[0] == frames:
        o_ref[...] = state
    else:
        cols = o_ref.shape[1]
        turned = jnp.swapaxes(state.astype(jnp.float32), 0, 1).astype(state.dtype)
        for r in range(o_ref.shape[0]):
            o_ref[r] = turned[r * pitch : r * pitch + cols]


def block(x, weight, kernel, proj, mask, pitch, cols=None):
    frames, length, chans = x.shape
    count = length - 2 * pitch
    shape = (frames, count, chans) if cols is None else (count // pitch, cols, frames, chans)
    dtype = x.dtype if cols is None else jnp.bfloat16
    flops = 2 * frames * count * chans * chans * 10
    vmem = pltpu.VMEM
    return pl.pallas_call(
        functools.partial(block_kernel, count=count, pitch=pitch),
        out_shape=jax.ShapeDtypeStruct(shape, dtype),
        in_specs=[pl.BlockSpec(memory_space=vmem)] * 5,
        out_specs=pl.BlockSpec(memory_space=vmem),
        compiler_params=pltpu.CompilerParams(vmem_limit_bytes=48 * 1024 * 1024),
        cost_estimate=pl.CostEstimate(
            flops=flops,
            transcendentals=frames * count * chans,
            bytes_accessed=x.dtype.itemsize * frames * (length + count) * chans + 2 * 10 * chans * chans,
        ),
    )(x, weight, kernel, proj, mask)


def shards(video, conv_w, depth_k, proj_w):
    bands = lax.axis_size("tm")
    sides = lax.axis_size("width")
    band = lax.axis_index("tm")
    side = lax.axis_index("width")
    frames, height, cols, chans = video.shape
    rows = height // bands
    halo = BLOCKS
    pitch = -(-(cols + 2 * halo) // LANES) * LANES

    pieces = jnp.zeros((bands, frames, rows + 2 * halo, cols, chans), video.dtype)
    for r in range(bands):
        first, last = max(r * rows - halo, 0), min(r * rows + rows + halo, height)
        start = first - (r * rows - halo)
        pieces = lax.dynamic_update_slice(pieces, video[None, :, first:last], (r, 0, start, 0, 0))
    received = lax.all_to_all(pieces, "tm", 0, 0, tiled=False)

    up = [(i, i + 1) for i in range(sides - 1)]
    down = [(i + 1, i) for i in range(sides - 1)]
    before = lax.ppermute(received[:, :, :, cols - halo :], "width", up)
    after = lax.ppermute(received[:, :, :, :halo], "width", down)
    def image_mask(left, width, first):
        n_rows = rows + 2 * left
        row = band * rows - left + lax.broadcasted_iota(jnp.int32, (n_rows, width), 0)
        col = side * cols + first + lax.broadcasted_iota(jnp.int32, (n_rows, width), 1)
        inside = (row >= 0) & (row < height) & (col >= 0) & (col < sides * cols)
        return jnp.broadcast_to(inside.reshape(-1, 1), (n_rows * width, chans)).astype(jnp.float32)

    band_in = jnp.pad(received, ((0, 0), (0, 0), (0, 0), (halo, pitch - cols - halo), (0, 0)))
    band_in = band_in.reshape(bands * frames, -1, chans)
    cut = (jnp.arange(pitch) < cols + 2 * (halo - 1)).astype(jnp.float32)
    first_mask = image_mask(halo - 1, pitch, -(halo - 1)) * jnp.tile(cut, rows + 2 * (halo - 1))[:, None]
    state = block(band_in, conv_w[0], depth_k[0], proj_w[0], first_mask, pitch)

    reach = 2 * halo
    late, before = lax.optimization_barrier((received, before))
    rim = jnp.concatenate([late[:, :, :, :halo], late[:, :, :, cols - halo :]], axis=3).astype(jnp.float32)
    rim = jnp.pad(rim, ((0, 0), (0, 0), (0, 0), (halo, halo), (0, 0)))
    rim = rim.reshape((bands * frames,) + rim.shape[2:])
    edge = (bands * frames, rows + 2 * halo, halo, chans)
    rim = lax.dynamic_update_slice(rim, before.astype(jnp.float32).reshape(edge), (0, 0, 0, 0))
    rim = lax.dynamic_update_slice(rim, after.astype(jnp.float32).reshape(edge), (0, 0, 3 * halo, 0))
    rim = rim.reshape(bands * frames, -1, chans)
    rim_left = image_mask(halo - 1, halo, -(halo - 1))
    rim_right = image_mask(halo - 1, halo, cols - 1)
    n_rows = rows + 2 * (halo - 1)
    rim_mask = jnp.concatenate(
        [rim_left.reshape(n_rows, halo, chans), jnp.zeros((n_rows, halo, chans), jnp.float32),
         rim_right.reshape(n_rows, halo, chans), jnp.zeros((n_rows, halo, chans), jnp.float32)], axis=1
    ).reshape(-1, chans)
    rims = block(rim, conv_w[0], depth_k[0], proj_w[0], rim_mask, 2 * reach)
    rims = rims.astype(state.dtype).reshape(bands * frames, n_rows, 2 * reach, chans)
    state = state.reshape(bands * frames, n_rows, pitch, chans)
    state = lax.dynamic_update_slice(state, rims[:, :, :halo], (0, 0, 0, 0))
    state = lax.dynamic_update_slice(state, rims[:, :, reach : reach + halo], (0, 0, cols + halo - 2 * (halo - 1), 0))
    state = state.reshape(bands * frames, -1, chans)

    for b in range(1, BLOCKS):
        left = halo - 1 - b
        mask = image_mask(left, pitch, -left)
        last = b == BLOCKS - 1
        state = block(state, conv_w[b], depth_k[b], proj_w[b], mask, pitch, cols if last else None)

    state = state.reshape(rows, cols, bands, frames, chans)
    state = jnp.transpose(state, (2, 0, 1, 3, 4))
    state = lax.all_to_all(state, "tm", 0, 1, tiled=True)
    return jnp.transpose(state[0], (2, 0, 1, 3))


def solution(mesh):
    return jax.shard_map(
        shards,
        mesh=mesh,
        in_specs=(P(("groups", "tm"), None, "width", None), P(), P(), P()),
        out_specs=P(("groups", "tm"), None, "width", None),
        check_vma=False,
    )
```

```python
import functools

import jax
import jax.numpy as jnp
from jax import lax
from jax.experimental import pallas as pl
from jax.experimental.pallas import tpu as pltpu
from jax.sharding import PartitionSpec as P

BLOCKS = 2
LANES = 16


def block_kernel(x_ref, w_ref, k_ref, p_ref, m_ref, o_ref, *, count, pitch, index):
    frames, _, chans = x_ref.shape
    total = frames * count

    def window(dy):
        return x_ref[:, dy * pitch : dy * pitch + count, :].reshape(total, chans)

    def operand(dy):
        return window(dy).astype(jnp.bfloat16)

    taps = [None, None, None]
    for dy in range(3):
        piece = operand(dy)
        for dx in range(3):
            part = jnp.dot(piece, w_ref[index, dy, dx], preferred_element_type=jnp.float32)
            taps[dx] = part if taps[dx] is None else taps[dx] + part
    conv = taps[0] + pltpu.roll(taps[1], total - 1, 0) + pltpu.roll(taps[2], total - 2, 0)
    hidden = (conv * (0.5 + 0.5 * jnp.tanh(0.5 * conv))).astype(jnp.bfloat16)

    values = hidden.astype(jnp.float32).reshape(frames, count, chans)
    kernel = k_ref[...]
    depth = []
    for t in range(frames):
        acc = values[t] * kernel[0:1]
        for lag in range(1, t + 1):
            acc = acc + values[t - lag] * kernel[lag : lag + 1]
        depth.append(acc.astype(jnp.bfloat16) if count % 16 == 0 else acc)
    depth = jnp.stack(depth).reshape(total, chans).astype(jnp.bfloat16)

    mixed = jnp.dot(depth, p_ref[...], preferred_element_type=jnp.float32).astype(jnp.bfloat16)
    center = pltpu.roll(window(1).astype(jnp.float32), total - 1, 0)
    state = (center + mixed.astype(jnp.float32)).astype(jnp.bfloat16).astype(o_ref.dtype)
    state = state.reshape(frames, count, chans)
    state = jnp.where(m_ref[...][None] > 0, state, jnp.zeros((), state.dtype))
    if o_ref.shape[0] == frames:
        o_ref[...] = state
    else:
        cols = o_ref.shape[1]
        turned = jnp.swapaxes(state.astype(jnp.float32), 0, 1).astype(state.dtype)
        for r in range(o_ref.shape[0]):
            o_ref[r] = turned[r * pitch : r * pitch + cols]


def block(x, weights, index, kernel, proj, mask, pitch, cols=None):
    frames, length, chans = x.shape
    count = length - 2 * pitch
    shape = (frames, count, chans) if cols is None else (count // pitch, cols, frames, chans)
    dtype = x.dtype if cols is None else jnp.bfloat16
    flops = 2 * frames * count * chans * chans * 10
    vmem = pltpu.VMEM
    return pl.pallas_call(
        functools.partial(block_kernel, count=count, pitch=pitch, index=index),
        out_shape=jax.ShapeDtypeStruct(shape, dtype),
        in_specs=[pl.BlockSpec(memory_space=vmem)] * 5,
        out_specs=pl.BlockSpec(memory_space=vmem),
        compiler_params=pltpu.CompilerParams(vmem_limit_bytes=48 * 1024 * 1024),
        cost_estimate=pl.CostEstimate(
            flops=flops,
            transcendentals=frames * count * chans,
            bytes_accessed=x.dtype.itemsize * frames * (length + count) * chans + 2 * 10 * chans * chans,
        ),
    )(x, weights, kernel, proj, mask)


def shards(video, conv_w, depth_k, proj_w):
    bands = lax.axis_size("tm")
    sides = lax.axis_size("width")
    band = lax.axis_index("tm")
    side = lax.axis_index("width")
    frames, height, cols, chans = video.shape
    rows = height // bands
    halo = BLOCKS
    pitch = -(-(cols + 2 * halo) // LANES) * LANES

    padded = jnp.pad(video, ((0, 0), (halo, halo), (0, 0), (0, 0)))
    pieces = jnp.stack([padded[:, r * rows : r * rows + rows + 2 * halo] for r in range(bands)])
    received = lax.all_to_all(pieces, "tm", 0, 0, tiled=False)

    up = [(i, i + 1) for i in range(sides - 1)]
    down = [(i + 1, i) for i in range(sides - 1)]
    before = lax.ppermute(received[:, :, :, cols - halo :], "width", up)
    after = lax.ppermute(received[:, :, :, :halo], "width", down)
    def image_mask(left, width, first):
        n_rows = rows + 2 * left
        row = band * rows - left + lax.broadcasted_iota(jnp.int32, (n_rows, width), 0)
        col = side * cols + first + lax.broadcasted_iota(jnp.int32, (n_rows, width), 1)
        inside = (row >= 0) & (row < height) & (col >= 0) & (col < sides * cols)
        return jnp.broadcast_to(inside.reshape(-1, 1), (n_rows * width, chans)).astype(jnp.float32)

    band_in = jnp.pad(received, ((0, 0), (0, 0), (0, 0), (halo, pitch - cols - halo), (0, 0)))
    band_in = band_in.reshape(bands * frames, -1, chans)
    cut = (jnp.arange(pitch) < cols + 2 * (halo - 1)).astype(jnp.float32)
    first_mask = image_mask(halo - 1, pitch, -(halo - 1)) * jnp.tile(cut, rows + 2 * (halo - 1))[:, None]
    state = block(band_in, conv_w, 0, depth_k[0], proj_w[0], first_mask, pitch)

    reach = 2 * halo
    late, before = lax.optimization_barrier((received, before))
    rim = jnp.concatenate([late[:, :, :, :halo], late[:, :, :, cols - halo :]], axis=3).astype(jnp.float32)
    rim = jnp.pad(rim, ((0, 0), (0, 0), (0, 0), (halo, halo), (0, 0)))
    rim = rim.reshape((bands * frames,) + rim.shape[2:])
    edge = (bands * frames, rows + 2 * halo, halo, chans)
    rim = lax.dynamic_update_slice(rim, before.astype(jnp.float32).reshape(edge), (0, 0, 0, 0))
    rim = lax.dynamic_update_slice(rim, after.astype(jnp.float32).reshape(edge), (0, 0, 3 * halo, 0))
    rim = rim.reshape(bands * frames, -1, chans)
    rim_left = image_mask(halo - 1, halo, -(halo - 1))
    rim_right = image_mask(halo - 1, halo, cols - 1)
    n_rows = rows + 2 * (halo - 1)
    rim_mask = jnp.concatenate(
        [rim_left.reshape(n_rows, halo, chans), jnp.zeros((n_rows, halo, chans), jnp.float32),
         rim_right.reshape(n_rows, halo, chans), jnp.zeros((n_rows, halo, chans), jnp.float32)], axis=1
    ).reshape(-1, chans)
    rims = block(rim, conv_w, 0, depth_k[0], proj_w[0], rim_mask, 2 * reach)
    rims = rims.astype(state.dtype).reshape(bands * frames, n_rows, 2 * reach, chans)
    state = state.reshape(bands * frames, n_rows, pitch, chans)
    state = lax.dynamic_update_slice(state, rims[:, :, :halo], (0, 0, 0, 0))
    state = lax.dynamic_update_slice(state, rims[:, :, reach : reach + halo], (0, 0, cols + halo - 2 * (halo - 1), 0))
    state = state.reshape(bands * frames, -1, chans)

    for b in range(1, BLOCKS):
        left = halo - 1 - b
        mask = image_mask(left, pitch, -left)
        last = b == BLOCKS - 1
        state = block(state, conv_w, b, depth_k[b], proj_w[b], mask, pitch, cols if last else None)

    state = state.reshape(rows, cols, bands, frames, chans)
    state = jnp.transpose(state, (2, 0, 1, 3, 4))
    state = lax.all_to_all(state, "tm", 0, 1, tiled=True)
    return jnp.transpose(state[0], (2, 0, 1, 3))


def solution(mesh):
    return jax.shard_map(
        shards,
        mesh=mesh,
        in_specs=(P(("groups", "tm"), None, "width", None), P(), P(), P()),
        out_specs=P(("groups", "tm"), None, "width", None),
        check_vma=False,
    )
```

```python
import functools

import jax
import jax.numpy as jnp
from jax import lax
from jax.experimental import pallas as pl
from jax.experimental.pallas import tpu as pltpu
from jax.sharding import PartitionSpec as P

BLOCKS = 2
LANES = 16


def block_kernel(x_ref, w_ref, k_ref, p_ref, *refs, count, pitch, index):
    m_ref, o_ref = refs if len(refs) == 2 else (None,) + refs
    frames, _, chans = x_ref.shape
    total = frames * count

    def window(dy):
        return x_ref[:, dy * pitch : dy * pitch + count, :].reshape(total, chans)

    def operand(dy):
        return window(dy).astype(jnp.bfloat16)

    taps = [None, None, None]
    for dy in range(3):
        piece = operand(dy)
        for dx in range(3):
            part = jnp.dot(piece, w_ref[index, dy, dx], preferred_element_type=jnp.float32)
            taps[dx] = part if taps[dx] is None else taps[dx] + part
    conv = taps[0] + pltpu.roll(taps[1], total - 1, 0) + pltpu.roll(taps[2], total - 2, 0)
    hidden = (conv * (0.5 + 0.5 * jnp.tanh(0.5 * conv))).astype(jnp.bfloat16)

    values = hidden.astype(jnp.float32).reshape(frames, count, chans)
    kernel = k_ref[...]
    depth = []
    for t in range(frames):
        acc = values[t] * kernel[0:1]
        for lag in range(1, t + 1):
            acc = acc + values[t - lag] * kernel[lag : lag + 1]
        depth.append(acc.astype(jnp.bfloat16) if count % 16 == 0 else acc)
    depth = jnp.stack(depth).reshape(total, chans).astype(jnp.bfloat16)

    mixed = jnp.dot(depth, p_ref[...], preferred_element_type=jnp.float32).astype(jnp.bfloat16)
    center = pltpu.roll(window(1).astype(jnp.float32), total - 1, 0)
    state = (center + mixed.astype(jnp.float32)).astype(jnp.bfloat16).astype(o_ref.dtype)
    state = state.reshape(frames, count, chans)
    if m_ref is not None:
        state = jnp.where(m_ref[...][None] > 0, state, jnp.zeros((), state.dtype))
    if o_ref.shape[0] == frames:
        o_ref[...] = state
    else:
        cols = o_ref.shape[1]
        turned = jnp.swapaxes(state.astype(jnp.float32), 0, 1).astype(state.dtype)
        for r in range(o_ref.shape[0]):
            o_ref[r] = turned[r * pitch : r * pitch + cols]


def block(x, weights, index, kernel, proj, mask, pitch, cols=None):
    frames, length, chans = x.shape
    count = length - 2 * pitch
    shape = (frames, count, chans) if cols is None else (count // pitch, cols, frames, chans)
    dtype = x.dtype if cols is None else jnp.bfloat16
    flops = 2 * frames * count * chans * chans * 10
    vmem = pltpu.VMEM
    return pl.pallas_call(
        functools.partial(block_kernel, count=count, pitch=pitch, index=index),
        out_shape=jax.ShapeDtypeStruct(shape, dtype),
        in_specs=[pl.BlockSpec(memory_space=vmem)] * (4 + (mask is not None)),
        out_specs=pl.BlockSpec(memory_space=vmem),
        compiler_params=pltpu.CompilerParams(vmem_limit_bytes=48 * 1024 * 1024),
        cost_estimate=pl.CostEstimate(
            flops=flops,
            transcendentals=frames * count * chans,
            bytes_accessed=x.dtype.itemsize * frames * (length + count) * chans + 2 * 10 * chans * chans,
        ),
    )(x, weights, kernel, proj, *([] if mask is None else [mask]))


def shards(video, conv_w, depth_k, proj_w):
    bands = lax.axis_size("tm")
    sides = lax.axis_size("width")
    band = lax.axis_index("tm")
    side = lax.axis_index("width")
    frames, height, cols, chans = video.shape
    rows = height // bands
    halo = BLOCKS
    pitch = -(-(cols + 2 * halo) // LANES) * LANES

    padded = jnp.pad(video, ((0, 0), (halo, halo), (0, 0), (0, 0)))
    pieces = jnp.stack([padded[:, r * rows : r * rows + rows + 2 * halo] for r in range(bands)])
    received = lax.all_to_all(pieces, "tm", 0, 0, tiled=False)

    up = [(i, i + 1) for i in range(sides - 1)]
    down = [(i + 1, i) for i in range(sides - 1)]
    before = lax.ppermute(received[:, :, :, cols - halo :], "width", up)
    after = lax.ppermute(received[:, :, :, :halo], "width", down)
    def image_mask(left, width, first):
        n_rows = rows + 2 * left
        row = band * rows - left + lax.broadcasted_iota(jnp.int32, (n_rows, width), 0)
        col = side * cols + first + lax.broadcasted_iota(jnp.int32, (n_rows, width), 1)
        inside = (row >= 0) & (row < height) & (col >= 0) & (col < sides * cols)
        return jnp.broadcast_to(inside.reshape(-1, 1), (n_rows * width, chans)).astype(jnp.float32)

    band_in = jnp.pad(received, ((0, 0), (0, 0), (0, 0), (halo, pitch - cols - halo), (0, 0)))
    band_in = band_in.reshape(bands * frames, -1, chans)
    cut = (jnp.arange(pitch) < cols + 2 * (halo - 1)).astype(jnp.float32)
    first_mask = image_mask(halo - 1, pitch, -(halo - 1)) * jnp.tile(cut, rows + 2 * (halo - 1))[:, None]
    state = block(band_in, conv_w, 0, depth_k[0], proj_w[0], first_mask, pitch)

    reach = 2 * halo
    late, before = lax.optimization_barrier((received, before))
    rim = jnp.concatenate([late[:, :, :, :halo], late[:, :, :, cols - halo :]], axis=3).astype(jnp.float32)
    rim = jnp.pad(rim, ((0, 0), (0, 0), (0, 0), (halo, halo), (0, 0)))
    rim = rim.reshape((bands * frames,) + rim.shape[2:])
    edge = (bands * frames, rows + 2 * halo, halo, chans)
    rim = lax.dynamic_update_slice(rim, before.astype(jnp.float32).reshape(edge), (0, 0, 0, 0))
    rim = lax.dynamic_update_slice(rim, after.astype(jnp.float32).reshape(edge), (0, 0, 3 * halo, 0))
    rim = rim.reshape(bands * frames, -1, chans)
    rim_left = image_mask(halo - 1, halo, -(halo - 1))
    rim_right = image_mask(halo - 1, halo, cols - 1)
    n_rows = rows + 2 * (halo - 1)
    rim_mask = jnp.concatenate(
        [rim_left.reshape(n_rows, halo, chans), jnp.zeros((n_rows, halo, chans), jnp.float32),
         rim_right.reshape(n_rows, halo, chans), jnp.zeros((n_rows, halo, chans), jnp.float32)], axis=1
    ).reshape(-1, chans)
    rims = block(rim, conv_w, 0, depth_k[0], proj_w[0], rim_mask, 2 * reach)
    rims = rims.astype(state.dtype).reshape(bands * frames, n_rows, 2 * reach, chans)
    state = state.reshape(bands * frames, n_rows, pitch, chans)
    state = lax.dynamic_update_slice(state, rims[:, :, :halo], (0, 0, 0, 0))
    state = lax.dynamic_update_slice(state, rims[:, :, reach : reach + halo], (0, 0, cols + halo - 2 * (halo - 1), 0))
    state = state.reshape(bands * frames, -1, chans)

    for b in range(1, BLOCKS):
        left = halo - 1 - b
        last = b == BLOCKS - 1
        mask = None if last else image_mask(left, pitch, -left)
        state = block(state, conv_w, b, depth_k[b], proj_w[b], mask, pitch, cols if last else None)

    state = state.reshape(rows, cols, bands, frames, chans)
    state = jnp.transpose(state, (2, 0, 1, 3, 4))
    state = lax.all_to_all(state, "tm", 0, 1, tiled=True)
    return jnp.transpose(state[0], (2, 0, 1, 3))


def solution(mesh):
    return jax.shard_map(
        shards,
        mesh=mesh,
        in_specs=(P(("groups", "tm"), None, "width", None), P(), P(), P()),
        out_specs=P(("groups", "tm"), None, "width", None),
        check_vma=False,
    )
```

```python
import functools

import jax
import jax.numpy as jnp
from jax import lax
from jax.experimental import pallas as pl
from jax.experimental.pallas import tpu as pltpu
from jax.sharding import PartitionSpec as P

BLOCKS = 2
LANES = 16


def block_kernel(x_ref, w_ref, k_ref, p_ref, *refs, count, pitch, index):
    m_ref, o_ref = refs if len(refs) == 2 else (None,) + refs
    frames, _, chans = x_ref.shape
    total = frames * count

    def window(dy):
        return x_ref[:, dy * pitch : dy * pitch + count, :].reshape(total, chans)

    def operand(dy):
        return window(dy).astype(jnp.bfloat16)

    taps = [None, None, None]
    for dy in range(3):
        piece = operand(dy)
        for dx in range(3):
            part = jnp.dot(piece, w_ref[index, dy, dx], preferred_element_type=jnp.float32)
            taps[dx] = part if taps[dx] is None else taps[dx] + part
    conv = taps[0] + pltpu.roll(taps[1], total - 1, 0) + pltpu.roll(taps[2], total - 2, 0)
    hidden = (conv * (0.5 + 0.5 * jnp.tanh(0.5 * conv))).astype(jnp.bfloat16)

    values = hidden.astype(jnp.float32).reshape(frames, count, chans)
    kernel = k_ref[index]
    depth = []
    for t in range(frames):
        acc = values[t] * kernel[0:1]
        for lag in range(1, t + 1):
            acc = acc + values[t - lag] * kernel[lag : lag + 1]
        depth.append(acc.astype(jnp.bfloat16) if count % 16 == 0 else acc)
    depth = jnp.stack(depth).reshape(total, chans).astype(jnp.bfloat16)

    mixed = jnp.dot(depth, p_ref[index], preferred_element_type=jnp.float32).astype(jnp.bfloat16)
    center = pltpu.roll(window(1).astype(jnp.float32), total - 1, 0)
    state = (center + mixed.astype(jnp.float32)).astype(jnp.bfloat16).astype(o_ref.dtype)
    state = state.reshape(frames, count, chans)
    if m_ref is not None:
        state = jnp.where(m_ref[...][None] > 0, state, jnp.zeros((), state.dtype))
    if o_ref.shape[0] == frames:
        o_ref[...] = state
    else:
        cols = o_ref.shape[1]
        turned = jnp.swapaxes(state.astype(jnp.float32), 0, 1).astype(state.dtype)
        for r in range(o_ref.shape[0]):
            o_ref[r] = turned[r * pitch : r * pitch + cols]


def block(x, weights, index, kernel, proj, mask, pitch, cols=None):
    frames, length, chans = x.shape
    count = length - 2 * pitch
    shape = (frames, count, chans) if cols is None else (count // pitch, cols, frames, chans)
    dtype = x.dtype if cols is None else jnp.bfloat16
    flops = 2 * frames * count * chans * chans * 10
    vmem = pltpu.VMEM
    return pl.pallas_call(
        functools.partial(block_kernel, count=count, pitch=pitch, index=index),
        out_shape=jax.ShapeDtypeStruct(shape, dtype),
        in_specs=[pl.BlockSpec(memory_space=vmem)] * (4 + (mask is not None)),
        out_specs=pl.BlockSpec(memory_space=vmem),
        compiler_params=pltpu.CompilerParams(vmem_limit_bytes=48 * 1024 * 1024),
        cost_estimate=pl.CostEstimate(
            flops=flops,
            transcendentals=frames * count * chans,
            bytes_accessed=x.dtype.itemsize * frames * (length + count) * chans + 2 * 10 * chans * chans,
        ),
    )(x, weights, kernel, proj, *([] if mask is None else [mask]))


def shards(video, conv_w, depth_k, proj_w):
    bands = lax.axis_size("tm")
    sides = lax.axis_size("width")
    band = lax.axis_index("tm")
    side = lax.axis_index("width")
    frames, height, cols, chans = video.shape
    rows = height // bands
    halo = BLOCKS
    pitch = -(-(cols + 2 * halo) // LANES) * LANES

    padded = jnp.pad(video, ((0, 0), (halo, halo), (0, 0), (0, 0)))
    pieces = jnp.stack([padded[:, r * rows : r * rows + rows + 2 * halo] for r in range(bands)])
    received = lax.all_to_all(pieces, "tm", 0, 0, tiled=False)

    up = [(i, i + 1) for i in range(sides - 1)]
    down = [(i + 1, i) for i in range(sides - 1)]
    before = lax.ppermute(received[:, :, :, cols - halo :], "width", up)
    after = lax.ppermute(received[:, :, :, :halo], "width", down)
    def image_mask(left, width, first):
        n_rows = rows + 2 * left
        row = band * rows - left + lax.broadcasted_iota(jnp.int32, (n_rows, width), 0)
        col = side * cols + first + lax.broadcasted_iota(jnp.int32, (n_rows, width), 1)
        inside = (row >= 0) & (row < height) & (col >= 0) & (col < sides * cols)
        return jnp.broadcast_to(inside.reshape(-1, 1), (n_rows * width, chans)).astype(jnp.float32)

    band_in = jnp.pad(received, ((0, 0), (0, 0), (0, 0), (halo, pitch - cols - halo), (0, 0)))
    band_in = band_in.reshape(bands * frames, -1, chans)
    cut = (jnp.arange(pitch) < cols + 2 * (halo - 1)).astype(jnp.float32)
    first_mask = image_mask(halo - 1, pitch, -(halo - 1)) * jnp.tile(cut, rows + 2 * (halo - 1))[:, None]
    state = block(band_in, conv_w, 0, depth_k, proj_w, first_mask, pitch)

    reach = 2 * halo
    late, before = lax.optimization_barrier((received, before))
    rim = jnp.concatenate([late[:, :, :, :halo], late[:, :, :, cols - halo :]], axis=3).astype(jnp.float32)
    rim = jnp.pad(rim, ((0, 0), (0, 0), (0, 0), (halo, halo), (0, 0)))
    rim = rim.reshape((bands * frames,) + rim.shape[2:])
    edge = (bands * frames, rows + 2 * halo, halo, chans)
    rim = lax.dynamic_update_slice(rim, before.astype(jnp.float32).reshape(edge), (0, 0, 0, 0))
    rim = lax.dynamic_update_slice(rim, after.astype(jnp.float32).reshape(edge), (0, 0, 3 * halo, 0))
    rim = rim.reshape(bands * frames, -1, chans)
    rim_left = image_mask(halo - 1, halo, -(halo - 1))
    rim_right = image_mask(halo - 1, halo, cols - 1)
    n_rows = rows + 2 * (halo - 1)
    rim_mask = jnp.concatenate(
        [rim_left.reshape(n_rows, halo, chans), jnp.zeros((n_rows, halo, chans), jnp.float32),
         rim_right.reshape(n_rows, halo, chans), jnp.zeros((n_rows, halo, chans), jnp.float32)], axis=1
    ).reshape(-1, chans)
    rims = block(rim, conv_w, 0, depth_k, proj_w, rim_mask, 2 * reach)
    rims = rims.astype(state.dtype).reshape(bands * frames, n_rows, 2 * reach, chans)
    state = state.reshape(bands * frames, n_rows, pitch, chans)
    state = lax.dynamic_update_slice(state, rims[:, :, :halo], (0, 0, 0, 0))
    state = lax.dynamic_update_slice(state, rims[:, :, reach : reach + halo], (0, 0, cols + halo - 2 * (halo - 1), 0))
    state = state.reshape(bands * frames, -1, chans)

    for b in range(1, BLOCKS):
        left = halo - 1 - b
        last = b == BLOCKS - 1
        mask = None if last else image_mask(left, pitch, -left)
        state = block(state, conv_w, b, depth_k, proj_w, mask, pitch, cols if last else None)

    state = state.reshape(rows, cols, bands, frames, chans)
    state = jnp.transpose(state, (2, 0, 1, 3, 4))
    state = lax.all_to_all(state, "tm", 0, 1, tiled=True)
    return jnp.transpose(state[0], (2, 0, 1, 3))


def solution(mesh):
    return jax.shard_map(
        shards,
        mesh=mesh,
        in_specs=(P(("groups", "tm"), None, "width", None), P(), P(), P()),
        out_specs=P(("groups", "tm"), None, "width", None),
        check_vma=False,
    )
```

```python
import functools

import jax
import jax.numpy as jnp
from jax import lax
from jax.experimental import pallas as pl
from jax.experimental.pallas import tpu as pltpu
from jax.sharding import PartitionSpec as P

BLOCKS = 2
LANES = 16


def block_kernel(x_ref, w_ref, k_ref, p_ref, *refs, count, pitch, index):
    m_ref, o_ref = refs if len(refs) == 2 else (None,) + refs
    frames, _, chans = x_ref.shape
    total = frames * count

    def window(dy):
        return x_ref[:, dy * pitch : dy * pitch + count, :].reshape(total, chans)

    def operand(dy):
        return window(dy).astype(jnp.bfloat16)

    taps = [None, None, None]
    for dy in range(3):
        piece = operand(dy)
        for dx in range(3):
            part = jnp.dot(piece, w_ref[index, dy, dx], preferred_element_type=jnp.float32)
            taps[dx] = part if taps[dx] is None else taps[dx] + part
    conv = taps[0] + pltpu.roll(taps[1], total - 1, 0) + pltpu.roll(taps[2], total - 2, 0)
    hidden = (conv * (0.5 + 0.5 * jnp.tanh(0.5 * conv))).astype(jnp.bfloat16)

    values = hidden.astype(jnp.float32).reshape(frames, count, chans)
    kernel = k_ref[...]
    depth = []
    for t in range(frames):
        acc = values[t] * kernel[0:1]
        for lag in range(1, t + 1):
            acc = acc + values[t - lag] * kernel[lag : lag + 1]
        depth.append(acc.astype(jnp.bfloat16) if count % 16 == 0 else acc)
    depth = jnp.stack(depth).reshape(total, chans).astype(jnp.bfloat16)

    mixed = jnp.dot(depth, p_ref[...], preferred_element_type=jnp.float32).astype(jnp.bfloat16)
    center = pltpu.roll(window(1).astype(jnp.float32), total - 1, 0)
    state = (center + mixed.astype(jnp.float32)).astype(jnp.bfloat16).astype(o_ref.dtype)
    state = state.reshape(frames, count, chans)
    if m_ref is not None:
        state = jnp.where(m_ref[...][None] > 0, state, jnp.zeros((), state.dtype))
    if o_ref.shape[0] == frames:
        o_ref[...] = state
    else:
        cols = o_ref.shape[1]
        turned = jnp.swapaxes(state.astype(jnp.float32), 0, 1).astype(state.dtype)
        for r in range(o_ref.shape[0]):
            o_ref[r] = turned[r * pitch : r * pitch + cols]


def block(x, weights, index, kernel, proj, mask, pitch, cols=None):
    frames, length, chans = x.shape
    count = length - 2 * pitch
    shape = (frames, count, chans) if cols is None else (count // pitch, cols, frames, chans)
    dtype = x.dtype if cols is None else jnp.bfloat16
    flops = 2 * frames * count * chans * chans * 10
    vmem = pltpu.VMEM
    return pl.pallas_call(
        functools.partial(block_kernel, count=count, pitch=pitch, index=index),
        out_shape=jax.ShapeDtypeStruct(shape, dtype),
        in_specs=[pl.BlockSpec(memory_space=vmem)] * (4 + (mask is not None)),
        out_specs=pl.BlockSpec(memory_space=vmem),
        compiler_params=pltpu.CompilerParams(vmem_limit_bytes=48 * 1024 * 1024),
        cost_estimate=pl.CostEstimate(
            flops=flops,
            transcendentals=frames * count * chans,
            bytes_accessed=x.dtype.itemsize * frames * (length + count) * chans + 2 * 10 * chans * chans,
        ),
    )(x, weights, kernel, proj, *([] if mask is None else [mask]))


def shards(video, conv_w, depth_k, proj_w):
    bands = lax.axis_size("tm")
    sides = lax.axis_size("width")
    band = lax.axis_index("tm")
    side = lax.axis_index("width")
    frames, height, cols, chans = video.shape
    rows = height // bands
    halo = BLOCKS
    pitch = -(-(cols + 2 * halo) // LANES) * LANES

    def band_rows(r):
        first, last = max(r * rows - halo, 0), min(r * rows + rows + halo, height)
        pad = ((0, 0), (first - (r * rows - halo), r * rows + rows + halo - last), (0, 0), (0, 0))
        return jnp.pad(video[:, first:last], pad)

    pieces = jnp.stack([band_rows(r) for r in range(bands)])
    received = lax.all_to_all(pieces, "tm", 0, 0, tiled=False)

    up = [(i, i + 1) for i in range(sides - 1)]
    down = [(i + 1, i) for i in range(sides - 1)]
    before = lax.ppermute(received[:, :, :, cols - halo :], "width", up)
    after = lax.ppermute(received[:, :, :, :halo], "width", down)
    def image_mask(left, width, first):
        n_rows = rows + 2 * left
        row = band * rows - left + lax.broadcasted_iota(jnp.int32, (n_rows, width), 0)
        col = side * cols + first + lax.broadcasted_iota(jnp.int32, (n_rows, width), 1)
        inside = (row >= 0) & (row < height) & (col >= 0) & (col < sides * cols)
        return jnp.broadcast_to(inside.reshape(-1, 1), (n_rows * width, chans)).astype(jnp.float32)

    band_in = jnp.pad(received, ((0, 0), (0, 0), (0, 0), (halo, pitch - cols - halo), (0, 0)))
    band_in = band_in.reshape(bands * frames, -1, chans)
    cut = (jnp.arange(pitch) < cols + 2 * (halo - 1)).astype(jnp.float32)
    first_mask = image_mask(halo - 1, pitch, -(halo - 1)) * jnp.tile(cut, rows + 2 * (halo - 1))[:, None]
    state = block(band_in, conv_w, 0, depth_k[0], proj_w[0], first_mask, pitch)

    reach = 2 * halo
    late, before = lax.optimization_barrier((received, before))
    rim = jnp.concatenate([late[:, :, :, :halo], late[:, :, :, cols - halo :]], axis=3).astype(jnp.float32)
    rim = jnp.pad(rim, ((0, 0), (0, 0), (0, 0), (halo, halo), (0, 0)))
    rim = rim.reshape((bands * frames,) + rim.shape[2:])
    edge = (bands * frames, rows + 2 * halo, halo, chans)
    rim = lax.dynamic_update_slice(rim, before.astype(jnp.float32).reshape(edge), (0, 0, 0, 0))
    rim = lax.dynamic_update_slice(rim, after.astype(jnp.float32).reshape(edge), (0, 0, 3 * halo, 0))
    rim = rim.reshape(bands * frames, -1, chans)
    rim_left = image_mask(halo - 1, halo, -(halo - 1))
    rim_right = image_mask(halo - 1, halo, cols - 1)
    n_rows = rows + 2 * (halo - 1)
    rim_mask = jnp.concatenate(
        [rim_left.reshape(n_rows, halo, chans), jnp.zeros((n_rows, halo, chans), jnp.float32),
         rim_right.reshape(n_rows, halo, chans), jnp.zeros((n_rows, halo, chans), jnp.float32)], axis=1
    ).reshape(-1, chans)
    rims = block(rim, conv_w, 0, depth_k[0], proj_w[0], rim_mask, 2 * reach)
    rims = rims.astype(state.dtype).reshape(bands * frames, n_rows, 2 * reach, chans)
    state = state.reshape(bands * frames, n_rows, pitch, chans)
    state = lax.dynamic_update_slice(state, rims[:, :, :halo], (0, 0, 0, 0))
    state = lax.dynamic_update_slice(state, rims[:, :, reach : reach + halo], (0, 0, cols + halo - 2 * (halo - 1), 0))
    state = state.reshape(bands * frames, -1, chans)

    for b in range(1, BLOCKS):
        left = halo - 1 - b
        last = b == BLOCKS - 1
        mask = None if last else image_mask(left, pitch, -left)
        state = block(state, conv_w, b, depth_k[b], proj_w[b], mask, pitch, cols if last else None)

    state = state.reshape(rows, cols, bands, frames, chans)
    state = jnp.transpose(state, (2, 0, 1, 3, 4))
    state = lax.all_to_all(state, "tm", 0, 1, tiled=True)
    return jnp.transpose(state[0], (2, 0, 1, 3))


def solution(mesh):
    return jax.shard_map(
        shards,
        mesh=mesh,
        in_specs=(P(("groups", "tm"), None, "width", None), P(), P(), P()),
        out_specs=P(("groups", "tm"), None, "width", None),
        check_vma=False,
    )
```
